32 devices in a mesh: fsdp: 8 (over y, x, core), dp: 4 (over z).
Axes of the slice: x: 2, y: 2, z: 4, core: 2. Of those that a mesh axis runs over, the one named last changes fastest.
Arguments:
- tokens: bfloat16 [12288, 8192], P(('fsdp', 'dp')), may hold values from -6 to 6
- output_gradient: bfloat16 [12288, 1024], P(('fsdp', 'dp')), may hold values from -6 to 6
- frozen_value_weight: bfloat16 [8192, 1024], P('fsdp'), may hold values from -0.0625 to 0.0625
- adapter_down_maps: bfloat16 [32, 16, 8192], P(('fsdp', 'dp')), may hold values from -0.0625 to 0.0625
- adapter_up_maps: bfloat16 [32, 16, 1024], P(('fsdp', 'dp')), may hold values from -1.5 to 1.5
- block_tenant_ids: int32 [96], P(('fsdp', 'dp')), may hold values from 0 to 31, as said below
- block_live_rows: int32 [96], P(('fsdp', 'dp')), may hold values from 33 to 128, as said below
- tenant_owner_slot: int32 [32], replicated, may hold values from 0 to 31, as said below
Outputs:
- output: bfloat16 [12288, 1024], P(('fsdp', 'dp'))
- token_gradient: bfloat16 [12288, 8192], P(('fsdp', 'dp'))
- grad_down: bfloat16 [32, 16, 8192], P(('fsdp', 'dp'))
- grad_up: bfloat16 [32, 16, 1024], P(('fsdp', 'dp'))
The draws below stay inside these ranges and needn't reach their ends.
Inputs may be any that keep to these rules, and one draw needn't show every extreme that they name: `block_tenant_ids`: A block held by a device whose index along dp is d names a tenant t with tenant_owner_slot[t] mod (size of dp) = d; tenant_owner_slot is a permutation. `block_live_rows`: the first block of every device is full. `tenant_owner_slot`: each slot is named once.
All inputs are finite; a program needn't handle non-finite values.
Results may differ from the reference program's by a relative error of at most 0.01.
Values may be sent and summed in bfloat16 or wider, within the bound.
No kernel may reach another device: no remote copies, remote signals or barrier semaphores. Data moves between devices by JAX's collectives and lax.ppermute only.
A program may use at most 192 MiB of HBM per device.

```python
import jax
import jax.numpy as jnp
from jax import lax

MODEL_DIM = 8192
VALUE_DIM = 1024
ADAPTER_RANK = 16
BLOCK = 128
BLK_DEV = 3
GROUPS = 4
GROUP_ADP = 8
ADAPTER_COUNT = 32
NBLOCKS = 96
TOKENS = 12288
N_FSDP = 8
N_DP = 4


def owner_permutation(key):
    return jax.random.permutation(jax.random.fold_in(key, 7), ADAPTER_COUNT).astype(jnp.int32)


def draw_tenant_owner_slot(key, part):
    return owner_permutation(key)


def draw_block_tenant_ids(key, part):
    perm_table = owner_permutation(key)
    inverse_table = jnp.argsort(perm_table).astype(jnp.int32)
    block_index = jnp.arange(NBLOCKS, dtype=jnp.int32)
    group_index = block_index // BLK_DEV % GROUPS
    member_pick = jax.random.randint(jax.random.fold_in(key, 11), (NBLOCKS,), 0, GROUP_ADP).astype(jnp.int32)
    slot_pick = group_index + GROUPS * member_pick
    return inverse_table[slot_pick].astype(jnp.int32)


def draw_block_live_rows(key, part):
    block_index = jnp.arange(NBLOCKS, dtype=jnp.int32)
    row_pick = jax.random.randint(jax.random.fold_in(key, 13), (NBLOCKS,), BLOCK // 4 + 1, BLOCK + 1).astype(jnp.int32)
    return jnp.where(block_index % BLK_DEV == 0, BLOCK, row_pick).astype(jnp.int32)


def shard_levels(own_key, dims, pieces, least, largest):
    gain, own = 1.0, jax.random.fold_in(own_key, 6)
    for axis_at, blocks in pieces:
        draws = jnp.exp(jax.random.uniform(jax.random.fold_in(own, axis_at), (blocks,), jnp.float32, least / len(pieces), largest / len(pieces)))
        gain = gain * jnp.repeat(draws, dims[axis_at] // blocks).reshape([-1 if axis == axis_at else 1 for axis in range(len(dims))])
    return gain


def gaussian(rng, shape, spread, reach, split=(), kind=jnp.bfloat16):
    entries = spread * jax.random.normal(rng, shape, jnp.float32)
    if split:
        entries = entries * shard_levels(rng, shape, split, -0.22, 0.18)
    return jnp.clip(entries, -reach, reach).astype(kind)


def setup_inputs(seed: int = 0) -> dict:
    arg_keys = jax.random.split(jax.random.key(seed), 9)
    tokens = gaussian(arg_keys[0], (TOKENS, MODEL_DIM), 1.0, 6.0, ((0, 32),))
    output_gradient = gaussian(arg_keys[1], (TOKENS, VALUE_DIM), 1.0, 6.0, ((0, 32),))
    frozen_value_weight = gaussian(arg_keys[2], (MODEL_DIM, VALUE_DIM), MODEL_DIM ** -0.5, 0.0625, ((0, 8),))
    adapter_down_maps = gaussian(arg_keys[3], (ADAPTER_COUNT, ADAPTER_RANK, MODEL_DIM), MODEL_DIM ** -0.5, 0.0625, ((0, 32),))
    adapter_up_maps = gaussian(arg_keys[4], (ADAPTER_COUNT, ADAPTER_RANK, VALUE_DIM), ADAPTER_RANK ** -0.5, 1.5, ((0, 32),))
    block_tenant_ids = draw_block_tenant_ids(jax.random.fold_in(arg_keys[8], 71), 0)
    block_live_rows = draw_block_live_rows(jax.random.fold_in(arg_keys[8], 71), 0)
    tenant_owner_slot = draw_tenant_owner_slot(jax.random.fold_in(arg_keys[8], 71), 0)
    return dict(tokens=tokens, output_gradient=output_gradient, frozen_value_weight=frozen_value_weight, adapter_down_maps=adapter_down_maps, adapter_up_maps=adapter_up_maps, block_tenant_ids=block_tenant_ids, block_live_rows=block_live_rows, tenant_owner_slot=tenant_owner_slot)


ADAPTER_SCALE = 2.0


def reference(tokens, output_gradient, frozen_value_weight, adapter_down_maps, adapter_up_maps, block_tenant_ids, block_live_rows, tenant_owner_slot):
    slot_ids = tenant_owner_slot[block_tenant_ids].astype(jnp.int32)
    live_rows = (jnp.arange(BLOCK)[None, :] < block_live_rows[:, None]).astype(jnp.float32)
    token_blocks = tokens.reshape(NBLOCKS, BLOCK, MODEL_DIM)
    cot_blocks = output_gradient.reshape(NBLOCKS, BLOCK, VALUE_DIM)

    def per_block(items):
        rows_in, cotangent_input, single_slot, mask_one = items
        down_matrix = adapter_down_maps[single_slot]
        up_matrix = adapter_up_maps[single_slot]
        mask_column = mask_one[:, None]
        low_rank_state = (jnp.dot(rows_in, down_matrix.T, preferred_element_type=jnp.float32) * mask_column).astype(jnp.bfloat16)
        low_rank_gradient = (ADAPTER_SCALE * jnp.dot(cotangent_input, up_matrix.T, preferred_element_type=jnp.float32) * mask_column).astype(jnp.bfloat16)
        frozen_output = jnp.dot(rows_in, frozen_value_weight, preferred_element_type=jnp.float32)
        adapter_output = jnp.dot(low_rank_state, up_matrix, preferred_element_type=jnp.float32)
        output_block = (mask_column * (frozen_output + ADAPTER_SCALE * adapter_output)).astype(jnp.bfloat16)
        frozen_backward = jnp.dot(cotangent_input, frozen_value_weight.T, preferred_element_type=jnp.float32)
        adapter_backward = jnp.dot(low_rank_gradient, down_matrix, preferred_element_type=jnp.float32)
        backward_block = (mask_column * (frozen_backward + adapter_backward)).astype(jnp.bfloat16)
        partial_down = jnp.dot(low_rank_gradient.T, rows_in, preferred_element_type=jnp.float32)
        partial_up = ADAPTER_SCALE * jnp.dot(low_rank_state.T, cotangent_input, preferred_element_type=jnp.float32)
        return output_block, backward_block, partial_down, partial_up

    out_blocks, back_blocks, partial_down, partial_up = lax.map(per_block, (token_blocks, cot_blocks, slot_ids, live_rows))
    output = out_blocks.reshape(TOKENS, VALUE_DIM)
    token_gradient = back_blocks.reshape(TOKENS, MODEL_DIM)
    devices_all = N_FSDP * N_DP
    slots_dev = slot_ids.reshape(devices_all, BLK_DEV)
    down_dev = partial_down.reshape(devices_all, BLK_DEV, ADAPTER_RANK * MODEL_DIM)
    up_dev = partial_up.reshape(devices_all, BLK_DEV, ADAPTER_RANK * VALUE_DIM)

    def add_device(totals, items):
        slots_one, down_one, up_one = items
        onehot = (slots_one[:, None] == jnp.arange(ADAPTER_COUNT)[None, :]).astype(jnp.float32)
        term_down = jnp.dot(onehot.T, down_one, precision=lax.Precision.HIGHEST).astype(jnp.bfloat16)
        term_up = jnp.dot(onehot.T, up_one, precision=lax.Precision.HIGHEST).astype(jnp.bfloat16)
        return (totals[0] + term_down.astype(jnp.float32), totals[1] + term_up.astype(jnp.float32)), None

    start_sums = (jnp.zeros((ADAPTER_COUNT, ADAPTER_RANK * MODEL_DIM), jnp.float32), jnp.zeros((ADAPTER_COUNT, ADAPTER_RANK * VALUE_DIM), jnp.float32))
    sums_all, unused = lax.scan(add_device, start_sums, (slots_dev, down_dev, up_dev))
    grad_down = sums_all[0].reshape(ADAPTER_COUNT, ADAPTER_RANK, MODEL_DIM).astype(jnp.bfloat16)
    grad_up = sums_all[1].reshape(ADAPTER_COUNT, ADAPTER_RANK, VALUE_DIM).astype(jnp.bfloat16)
    return (output, token_gradient, grad_down, grad_up)
```

```python
import jax
import jax.numpy as jnp
from jax import lax
from jax.sharding import PartitionSpec as P

ADAPTER_SCALE = 2.0


def xor_pairs(count, step):
    return [(src, src ^ step) for src in range(count)]


def on_device(
    tokens,
    output_gradient,
    frozen_value_weight,
    adapter_down_maps,
    adapter_up_maps,
    block_tenant_ids,
    block_live_rows,
    tenant_owner_slot,
):
    tok_rows, model_width = tokens.shape
    value_width = output_gradient.shape[1]
    rank = adapter_down_maps.shape[1]
    blocks = block_tenant_ids.shape[0]
    block_length = tok_rows // blocks
    groups = lax.axis_size("dp")
    members = lax.axis_size("fsdp")
    shard_rows = frozen_value_weight.shape[0]
    me = lax.axis_index("fsdp")

    own_adapter = jnp.concatenate([adapter_down_maps[0], adapter_up_maps[0]], axis=1)
    gathered = [own_adapter]
    for step in range(1, members):
        gathered.append(lax.ppermute(own_adapter, "fsdp", xor_pairs(members, step)))
    adapter_stack = jnp.stack(gathered)

    slot_ids = jnp.take(tenant_owner_slot, block_tenant_ids)
    member_ids = slot_ids // groups
    picked = jnp.stack([lax.dynamic_index_in_dim(adapter_stack, me ^ member_ids[b], 0, keepdims=False)
                        for b in range(blocks)])
    down_block = picked[:, :, :model_width]
    up_block = picked[:, :, model_width:]

    live_rows = (jnp.arange(block_length)[None, :] < block_live_rows[:, None]).astype(jnp.float32)
    live_column = live_rows[:, :, None]
    token_blocks = tokens.reshape(blocks, block_length, model_width)
    cot_blocks = output_gradient.reshape(blocks, block_length, value_width)

    low_rank_state = (
        jnp.einsum("cvj,coj->cvo", token_blocks, down_block, preferred_element_type=jnp.float32)
        * live_column
    ).astype(jnp.bfloat16)
    low_rank_gradient = (
        ADAPTER_SCALE
        * jnp.einsum("btv,bkv->btk", cot_blocks, up_block, preferred_element_type=jnp.float32)
        * live_column
    ).astype(jnp.bfloat16)

    partial_down = jnp.einsum(
        "vio,vih->voh", low_rank_gradient, token_blocks, preferred_element_type=jnp.float32
    )
    partial_up = ADAPTER_SCALE * jnp.einsum(
        "btk,btv->bkv", low_rank_state, cot_blocks, preferred_element_type=jnp.float32
    )
    partial = jnp.concatenate([partial_down, partial_up], axis=2)

    def table_row(member):
        row = jnp.zeros(partial.shape[1:], jnp.float32)
        for b in range(blocks):
            row = row + jnp.where(member_ids[b] == member, partial[b], 0.0)
        return row.astype(jnp.bfloat16)

    grad_sum = table_row(me).astype(jnp.float32)
    for step in range(1, members):
        sent = table_row(me ^ step)
        grad_sum = grad_sum + lax.ppermute(sent, "fsdp", xor_pairs(members, step)).astype(jnp.float32)
    grad_sum = grad_sum.astype(jnp.bfloat16)
    grad_down = grad_sum[None, :, :model_width]
    grad_up = grad_sum[None, :, model_width:]

    weight_parts = {0: frozen_value_weight}
    for step in range(2, members, 2):
        weight_parts[step] = lax.ppermute(frozen_value_weight, "fsdp", xor_pairs(members, step))
    for step in range(0, members, 2):
        weight_parts[step + 1] = lax.ppermute(weight_parts[step], "fsdp", xor_pairs(members, 1))

    adapter_output = jnp.einsum(
        "znr,zrm->znm", low_rank_state, up_block, preferred_element_type=jnp.float32
    ).reshape(tok_rows, value_width)
    live_flat = live_rows.reshape(tok_rows, 1)
    masked_cot = (output_gradient * live_flat).astype(jnp.bfloat16)

    output_total = ADAPTER_SCALE * adapter_output
    token_gradient = jnp.zeros((tok_rows, model_width), jnp.bfloat16)
    for step in range(members):
        weight_piece = weight_parts[step]
        column = (me ^ step) * shard_rows
        token_piece = lax.dynamic_slice_in_dim(tokens, column, shard_rows, axis=1)
        output_total = output_total + jnp.dot(
            token_piece, weight_piece, preferred_element_type=jnp.float32
        )
        down_piece = lax.dynamic_slice_in_dim(down_block, column, shard_rows, axis=2)
        backward_piece = lax.dot_general(
            masked_cot, weight_piece, (((1,), (1,)), ((), ())), preferred_element_type=jnp.float32
        ) + jnp.einsum(
            "uio,uof->uif", low_rank_gradient, down_piece, preferred_element_type=jnp.float32
        ).reshape(tok_rows, shard_rows)
        token_gradient = lax.dynamic_update_slice_in_dim(
            token_gradient, backward_piece.astype(jnp.bfloat16), column, axis=1
        )
    output = (live_flat * output_total).astype(jnp.bfloat16)
    return (output, token_gradient, grad_down, grad_up)


def solution(mesh):
    placed = (
        P(("fsdp", "dp"), None),
        P(("fsdp", "dp"), None),
        P("fsdp", None),
        P(("fsdp", "dp"), None, None),
        P(("fsdp", "dp"), None, None),
        P(("fsdp", "dp")),
        P(("fsdp", "dp")),
        P(),
    )
    return jax.shard_map(
        on_device,
        mesh=mesh,
        in_specs=placed,
        out_specs=(
            P(("fsdp", "dp"), None),
            P(("fsdp", "dp"), None),
            P(("fsdp", "dp"), None, None),
            P(("fsdp", "dp"), None, None),
        ),
        check_vma=False,
    )
```

```python
import jax
import jax.numpy as jnp
from jax import lax
from jax.sharding import PartitionSpec as P

ADAPTER_SCALE = 2.0


def on_device(
    tokens,
    output_gradient,
    frozen_value_weight,
    adapter_down_maps,
    adapter_up_maps,
    block_tenant_ids,
    block_live_rows,
    tenant_owner_slot,
):
    tok_rows = tokens.shape[0]
    model_width_size = tokens.shape[1]
    value_width_size = output_gradient.shape[1]
    adapter_rank_size = adapter_down_maps.shape[1]
    number_of_blocks = block_tenant_ids.shape[0]
    block_length = tok_rows // number_of_blocks
    groups = lax.axis_size("dp")
    members = lax.axis_size("fsdp")
    tenant_ids = jnp.arange(tenant_owner_slot.shape[0], dtype=jnp.int32)
    slot_ids = jnp.sum(
        jnp.where(block_tenant_ids[:, None] == tenant_ids[None, :], tenant_owner_slot[None, :], 0),
        axis=1,
    )
    member_ids = slot_ids // groups
    live_rows = (jnp.arange(block_length)[None, :] < block_live_rows[:, None]).astype(jnp.float32)
    live_column = live_rows[:, :, None]
    down_all, up_all = (
        lax.all_gather(adapter_down_maps, "fsdp", axis=0, tiled=True),
        lax.all_gather(adapter_up_maps, "fsdp", axis=0, tiled=True),
    )
    onehot = (member_ids[:, None] == jnp.arange(members)[None, :]).astype(jnp.bfloat16)
    down_block = jnp.dot(onehot, down_all.reshape(members, -1), preferred_element_type=jnp.float32)
    down_block = down_block.astype(jnp.bfloat16).reshape(
        number_of_blocks, adapter_rank_size, model_width_size
    )
    up_block = jnp.dot(onehot, up_all.reshape(members, -1), preferred_element_type=jnp.float32)
    up_block = up_block.astype(jnp.bfloat16).reshape(
        number_of_blocks, adapter_rank_size, value_width_size
    )
    token_blocks = tokens.reshape(number_of_blocks, block_length, model_width_size)
    cot_blocks = output_gradient.reshape(number_of_blocks, block_length, value_width_size)
    low_rank_state = (
        jnp.einsum("cvj,coj->cvo", token_blocks, down_block, preferred_element_type=jnp.float32)
        * live_column
    ).astype(jnp.bfloat16)
    low_rank_gradient = (
        ADAPTER_SCALE
        * jnp.einsum("btv,bkv->btk", cot_blocks, up_block, preferred_element_type=jnp.float32)
        * live_column
    ).astype(jnp.bfloat16)
    adapter_output = jnp.einsum(
        "znr,zrm->znm", low_rank_state, up_block, preferred_element_type=jnp.float32
    )
    adapter_backward = jnp.einsum(
        "uio,uof->uif", low_rank_gradient, down_block, preferred_element_type=jnp.float32
    )
    quarter_rows = frozen_value_weight.shape[0] // groups
    weight_quarter = lax.dynamic_slice_in_dim(
        frozen_value_weight, lax.axis_index("dp") * quarter_rows, quarter_rows, axis=0
    )
    weight_piece = lax.all_gather(weight_quarter, ("fsdp", "dp"), axis=0, tiled=True)
    output_total = jnp.dot(tokens, weight_piece, preferred_element_type=jnp.float32)
    backward_piece = lax.dot_general(
        output_gradient, weight_piece, (((1,), (1,)), ((), ())), preferred_element_type=jnp.float32
    )
    output = live_column * (
        output_total.reshape(number_of_blocks, block_length, value_width_size)
        + ADAPTER_SCALE * adapter_output
    )
    output = output.astype(jnp.bfloat16).reshape(tok_rows, value_width_size)
    token_gradient = live_column * (
        backward_piece.reshape(number_of_blocks, block_length, model_width_size) + adapter_backward
    )
    token_gradient = token_gradient.astype(jnp.bfloat16).reshape(tok_rows, model_width_size)
    partial_down = jnp.einsum(
        "vio,vih->voh", low_rank_gradient, token_blocks, preferred_element_type=jnp.float32
    )
    partial_up = ADAPTER_SCALE * jnp.einsum(
        "btk,btv->bkv", low_rank_state, cot_blocks, preferred_element_type=jnp.float32
    )
    member_range = jnp.arange(members, dtype=jnp.int32)
    table_down = jnp.zeros((members, adapter_rank_size, model_width_size), jnp.float32)
    table_up = jnp.zeros((members, adapter_rank_size, value_width_size), jnp.float32)
    for block_num in range(number_of_blocks):
        picked = (member_range == member_ids[block_num]).astype(jnp.float32)[:, None, None]
        table_down = table_down + picked * partial_down[block_num][None]
        table_up = table_up + picked * partial_up[block_num][None]
    term_down = table_down.astype(jnp.bfloat16)
    term_up = table_up.astype(jnp.bfloat16)
    sum_down, sum_up = (
        lax.psum_scatter(
            term_down.astype(jnp.float32).astype(jnp.bfloat16),
            "fsdp",
            scatter_dimension=0,
            tiled=True,
        ).astype(jnp.float32),
        lax.psum_scatter(
            term_up.astype(jnp.float32).astype(jnp.bfloat16),
            "fsdp",
            scatter_dimension=0,
            tiled=True,
        ).astype(jnp.float32),
    )
    return (output, token_gradient, sum_down.astype(jnp.bfloat16), sum_up.astype(jnp.bfloat16))


def solution(mesh):
    placed = (
        P(("fsdp", "dp"), None),
        P(("fsdp", "dp"), None),
        P("fsdp", None),
        P(("fsdp", "dp"), None, None),
        P(("fsdp", "dp"), None, None),
        P(("fsdp", "dp")),
        P(("fsdp", "dp")),
        P(),
    )
    return jax.shard_map(
        on_device,
        mesh=mesh,
        in_specs=placed,
        out_specs=(
            P(("fsdp", "dp"), None),
            P(("fsdp", "dp"), None),
            P(("fsdp", "dp"), None, None),
            P(("fsdp", "dp"), None, None),
        ),
        check_vma=False,
    )
```

```python
import jax
import jax.numpy as jnp
from jax import lax
from jax.sharding import PartitionSpec as P

ADAPTER_SCALE = 2.0
WEIGHT_CHUNKS = 2


def xor_pairs(count, step):
    return [(src, src ^ step) for src in range(count)]


def relay_gather(shard, members, groups, me, dp_index):
    flat = members * groups
    parity = me % 2
    if members != 8 or groups % 2 != 0:
        parts = {0: shard}
        for step in range(2, members, 2):
            parts[step] = lax.ppermute(shard, "fsdp", xor_pairs(members, step))
        for step in range(0, members, 2):
            parts[step + 1] = lax.ppermute(parts[step], "fsdp", xor_pairs(members, 1))
        return [(me ^ step, parts[step]) for step in range(members)]

    def flat_pairs(target):
        pairs = []
        for i in range(members):
            for d in range(groups):
                role = (i % 2) ^ (d % 2)
                ti, td = target(i, d, role)
                pairs.append((i * groups + d, ti * groups + td))
        return pairs

    first_pairs = flat_pairs(lambda i, d, role: (i ^ (2 + 2 * role), d))
    relay_pairs = flat_pairs(lambda i, d, role: (i ^ (4 - 2 * role), d))
    partner_pairs = flat_pairs(lambda i, d, role: (i, d ^ 1))
    role = parity ^ (dp_index % 2)
    rows = shard.shape[0] // WEIGHT_CHUNKS
    chunks = []
    for k in range(WEIGHT_CHUNKS):
        piece = shard[k * rows:(k + 1) * rows]
        first = lax.ppermute(piece, ("fsdp", "dp"), first_pairs)
        relayed = lax.ppermute(first, ("fsdp", "dp"), relay_pairs)
        partner = lax.ppermute(first, ("fsdp", "dp"), partner_pairs)
        own_four = jnp.stack([piece, first, relayed, partner])
        sibling_four = lax.ppermute(own_four, "fsdp", xor_pairs(members, 1))
        chunks.append((piece, first, relayed, partner, sibling_four))
    sources = [me, me ^ (2 + 2 * role), me ^ 6, me ^ (4 - 2 * role)]
    sibling = me ^ 1
    sibling_role = 1 - role
    sibling_sources = [sibling, sibling ^ (2 + 2 * sibling_role), sibling ^ 6,
                       sibling ^ (4 - 2 * sibling_role)]
    result = []
    for k in range(WEIGHT_CHUNKS):
        piece, first, relayed, partner, sibling_four = chunks[k]
        for source, value in zip(sources, (piece, first, relayed, partner)):
            result.append((source, k, value))
        for index, source in enumerate(sibling_sources):
            result.append((source, k, sibling_four[index]))
    return result


def on_device(
    tokens,
    output_gradient,
    frozen_value_weight,
    adapter_down_maps,
    adapter_up_maps,
    block_tenant_ids,
    block_live_rows,
    tenant_owner_slot,
):
    tok_rows, model_width = tokens.shape
    value_width = output_gradient.shape[1]
    blocks = block_tenant_ids.shape[0]
    block_length = tok_rows // blocks
    groups = lax.axis_size("dp")
    members = lax.axis_size("fsdp")
    shard_rows = frozen_value_weight.shape[0]
    me = lax.axis_index("fsdp")
    dp_index = lax.axis_index("dp")
    even_steps = list(range(2, members, 2))

    own_adapter = jnp.concatenate([adapter_down_maps[0], adapter_up_maps[0]], axis=1)
    by_step = {0: own_adapter}
    for step in even_steps:
        by_step[step] = lax.ppermute(own_adapter, "fsdp", xor_pairs(members, step))
    same_parity = jnp.stack([by_step[step] for step in range(0, members, 2)])
    other_parity = lax.ppermute(same_parity, "fsdp", xor_pairs(members, 1))
    for index, step in enumerate(range(0, members, 2)):
        by_step[step ^ 1] = other_parity[index]
    adapter_stack = jnp.stack([by_step[step] for step in range(members)])

    slot_ids = jnp.take(tenant_owner_slot, block_tenant_ids)
    member_ids = slot_ids // groups
    picked = jnp.stack([lax.dynamic_index_in_dim(adapter_stack, me ^ member_ids[b], 0, keepdims=False)
                        for b in range(blocks)])
    down_block = picked[:, :, :model_width]
    up_block = picked[:, :, model_width:]

    live_rows = (jnp.arange(block_length)[None, :] < block_live_rows[:, None]).astype(jnp.float32)
    live_column = live_rows[:, :, None]
    token_blocks = tokens.reshape(blocks, block_length, model_width)
    cot_blocks = output_gradient.reshape(blocks, block_length, value_width)

    low_rank_state = (
        jnp.einsum("cvj,coj->cvo", token_blocks, down_block, preferred_element_type=jnp.float32)
        * live_column
    ).astype(jnp.bfloat16)
    low_rank_gradient = (
        ADAPTER_SCALE
        * jnp.einsum("btv,bkv->btk", cot_blocks, up_block, preferred_element_type=jnp.float32)
        * live_column
    ).astype(jnp.bfloat16)

    partial_down = jnp.einsum(
        "vio,vih->voh", low_rank_gradient, token_blocks, preferred_element_type=jnp.float32
    )
    partial_up = ADAPTER_SCALE * jnp.einsum(
        "btk,btv->bkv", low_rank_state, cot_blocks, preferred_element_type=jnp.float32
    )
    partial = jnp.concatenate([partial_down, partial_up], axis=2)

    def table_row(member):
        row = jnp.zeros(partial.shape[1:], jnp.float32)
        for b in range(blocks):
            row = row + jnp.where(member_ids[b] == member, partial[b], 0.0)
        return row.astype(jnp.bfloat16)

    sibling = me ^ 1
    for_sibling = jnp.stack([table_row(sibling ^ step) for step in range(0, members, 2)])
    from_sibling = lax.ppermute(for_sibling, "fsdp", xor_pairs(members, 1))
    pair_sums = [
        table_row(me ^ step).astype(jnp.float32) + from_sibling[index].astype(jnp.float32)
        for index, step in enumerate(range(0, members, 2))
    ]
    grad_sum = pair_sums[0]
    for index, step in enumerate(even_steps):
        sent = pair_sums[index + 1].astype(jnp.bfloat16)
        grad_sum = grad_sum + lax.ppermute(sent, "fsdp", xor_pairs(members, step)).astype(jnp.float32)
    grad_sum = grad_sum.astype(jnp.bfloat16)
    grad_down = grad_sum[None, :, :model_width]
    grad_up = grad_sum[None, :, model_width:]

    weight_pieces = relay_gather(frozen_value_weight, members, groups, me, dp_index)
    if weight_pieces and len(weight_pieces[0]) == 2:
        weight_pieces = [(source, 0, value) for source, value in weight_pieces]
    adapter_output = jnp.einsum(
        "znr,zrm->znm", low_rank_state, up_block, preferred_element_type=jnp.float32
    ).reshape(tok_rows, value_width)
    live_flat = live_rows.reshape(tok_rows, 1)
    masked_cot = (output_gradient * live_flat).astype(jnp.bfloat16)

    output_total = ADAPTER_SCALE * adapter_output
    token_gradient = jnp.zeros((tok_rows, model_width), jnp.bfloat16)
    for source, chunk, weight_piece in weight_pieces:
        piece_rows = weight_piece.shape[0]
        column = source * shard_rows + chunk * piece_rows
        token_piece = lax.dynamic_slice_in_dim(tokens, column, piece_rows, axis=1)
        output_total = output_total + jnp.dot(
            token_piece, weight_piece, preferred_element_type=jnp.float32
        )
        down_piece = lax.dynamic_slice_in_dim(down_block, column, piece_rows, axis=2)
        backward_piece = lax.dot_general(
            masked_cot, weight_piece, (((1,), (1,)), ((), ())), preferred_element_type=jnp.float32
        ) + jnp.einsum(
            "uio,uof->uif", low_rank_gradient, down_piece, preferred_element_type=jnp.float32
        ).reshape(tok_rows, piece_rows)
        token_gradient = lax.dynamic_update_slice_in_dim(
            token_gradient, backward_piece.astype(jnp.bfloat16), column, axis=1
        )
    output = (live_flat * output_total).astype(jnp.bfloat16)
    return (output, token_gradient, grad_down, grad_up)


def solution(mesh):
    placed = (
        P(("fsdp", "dp"), None),
        P(("fsdp", "dp"), None),
        P("fsdp", None),
        P(("fsdp", "dp"), None, None),
        P(("fsdp", "dp"), None, None),
        P(("fsdp", "dp")),
        P(("fsdp", "dp")),
        P(),
    )
    return jax.shard_map(
        on_device,
        mesh=mesh,
        in_specs=placed,
        out_specs=(
            P(("fsdp", "dp"), None),
            P(("fsdp", "dp"), None),
            P(("fsdp", "dp"), None, None),
            P(("fsdp", "dp"), None, None),
        ),
        check_vma=False,
    )
```

```python
import jax
import jax.numpy as jnp
from jax import lax
from jax.sharding import PartitionSpec as P

ADAPTER_SCALE = 2.0
WEIGHT_CHUNKS = 2


def xor_pairs(count, step):
    return [(src, src ^ step) for src in range(count)]


def relay_gather(shard, members, groups, me, dp_index):
    flat = members * groups
    parity = me % 2
    if members != 8 or groups % 2 != 0:
        parts = {0: shard}
        for step in range(2, members, 2):
            parts[step] = lax.ppermute(shard, "fsdp", xor_pairs(members, step))
        for step in range(0, members, 2):
            parts[step + 1] = lax.ppermute(parts[step], "fsdp", xor_pairs(members, 1))
        return [(me ^ step, parts[step]) for step in range(members)]

    def flat_pairs(target):
        pairs = []
        for i in range(members):
            for d in range(groups):
                role = (i % 2) ^ (d % 2)
                ti, td = target(i, d, role)
                pairs.append((i * groups + d, ti * groups + td))
        return pairs

    first_pairs = flat_pairs(lambda i, d, role: (i ^ (2 + 2 * role), d))
    relay_pairs = flat_pairs(lambda i, d, role: (i ^ (4 - 2 * role), d))
    partner_pairs = flat_pairs(lambda i, d, role: (i, d ^ 1))
    role = parity ^ (dp_index % 2)
    sibling = me ^ 1
    sibling_role = 1 - role
    sources = [me, me ^ (2 + 2 * role), me ^ 6, me ^ (4 - 2 * role)]
    sibling_sources = [sibling, sibling ^ (2 + 2 * sibling_role), sibling ^ 6,
                       sibling ^ (4 - 2 * sibling_role)]
    rows = shard.shape[0] // WEIGHT_CHUNKS
    result = []
    previous = None
    for k in range(WEIGHT_CHUNKS):
        piece = shard[k * rows:(k + 1) * rows]
        result.append((0.0, sources[0], k, piece))
        result.append((1.0, sibling_sources[0], k, lax.ppermute(piece, "fsdp", xor_pairs(members, 1))))
        if previous is not None:
            piece, _ = lax.optimization_barrier((piece, previous))
        first = lax.ppermute(piece, ("fsdp", "dp"), first_pairs)
        previous = first
        result.append((2.0 + 2 * k, sources[1], k, first))
        result.append((3.0 + 2 * k, sibling_sources[1], k, lax.ppermute(first, "fsdp", xor_pairs(members, 1))))
        relayed = lax.ppermute(first, ("fsdp", "dp"), relay_pairs)
        partner = lax.ppermute(first, ("fsdp", "dp"), partner_pairs)
        result.append((4.5 + 2 * k, sources[2], k, relayed))
        result.append((4.5 + 2 * k, sources[3], k, partner))
        late = lax.ppermute(jnp.stack([relayed, partner]), "fsdp", xor_pairs(members, 1))
        result.append((5.5 + 2 * k, sibling_sources[2], k, late[0]))
        result.append((5.5 + 2 * k, sibling_sources[3], k, late[1]))
    result.sort(key=lambda item: item[0])
    return [item[1:] for item in result]


def on_device(
    tokens,
    output_gradient,
    frozen_value_weight,
    adapter_down_maps,
    adapter_up_maps,
    block_tenant_ids,
    block_live_rows,
    tenant_owner_slot,
):
    tok_rows, model_width = tokens.shape
    value_width = output_gradient.shape[1]
    blocks = block_tenant_ids.shape[0]
    block_length = tok_rows // blocks
    groups = lax.axis_size("dp")
    members = lax.axis_size("fsdp")
    shard_rows = frozen_value_weight.shape[0]
    me = lax.axis_index("fsdp")
    dp_index = lax.axis_index("dp")
    even_steps = list(range(2, members, 2))

    own_adapter = jnp.concatenate([adapter_down_maps[0], adapter_up_maps[0]], axis=1)
    by_step = {0: own_adapter}
    for step in even_steps:
        by_step[step] = lax.ppermute(own_adapter, "fsdp", xor_pairs(members, step))
    same_parity = jnp.stack([by_step[step] for step in range(0, members, 2)])
    other_parity = lax.ppermute(same_parity, "fsdp", xor_pairs(members, 1))
    for index, step in enumerate(range(0, members, 2)):
        by_step[step ^ 1] = other_parity[index]
    adapter_stack = jnp.stack([by_step[step] for step in range(members)])

    slot_ids = jnp.take(tenant_owner_slot, block_tenant_ids)
    member_ids = slot_ids // groups
    picked = jnp.stack([lax.dynamic_index_in_dim(adapter_stack, me ^ member_ids[b], 0, keepdims=False)
                        for b in range(blocks)])
    down_block = picked[:, :, :model_width]
    up_block = picked[:, :, model_width:]

    live_rows = (jnp.arange(block_length)[None, :] < block_live_rows[:, None]).astype(jnp.float32)
    live_column = live_rows[:, :, None]
    token_blocks = tokens.reshape(blocks, block_length, model_width)
    cot_blocks = output_gradient.reshape(blocks, block_length, value_width)

    low_rank_state = (
        jnp.einsum("cvj,coj->cvo", token_blocks, down_block, preferred_element_type=jnp.float32)
        * live_column
    ).astype(jnp.bfloat16)
    low_rank_gradient = (
        ADAPTER_SCALE
        * jnp.einsum("btv,bkv->btk", cot_blocks, up_block, preferred_element_type=jnp.float32)
        * live_column
    ).astype(jnp.bfloat16)

    partial_down = jnp.einsum(
        "vio,vih->voh", low_rank_gradient, token_blocks, preferred_element_type=jnp.float32
    )
    partial_up = ADAPTER_SCALE * jnp.einsum(
        "btk,btv->bkv", low_rank_state, cot_blocks, preferred_element_type=jnp.float32
    )
    partial = jnp.concatenate([partial_down, partial_up], axis=2)

    def table_row(member):
        row = jnp.zeros(partial.shape[1:], jnp.float32)
        for b in range(blocks):
            row = row + jnp.where(member_ids[b] == member, partial[b], 0.0)
        return row.astype(jnp.bfloat16)

    sibling = me ^ 1
    for_sibling = jnp.stack([table_row(sibling ^ step) for step in range(0, members, 2)])
    from_sibling = lax.ppermute(for_sibling, "fsdp", xor_pairs(members, 1))
    pair_sums = [
        table_row(me ^ step).astype(jnp.float32) + from_sibling[index].astype(jnp.float32)
        for index, step in enumerate(range(0, members, 2))
    ]
    grad_sum = pair_sums[0]
    for index, step in enumerate(even_steps):
        sent = pair_sums[index + 1].astype(jnp.bfloat16)
        grad_sum = grad_sum + lax.ppermute(sent, "fsdp", xor_pairs(members, step)).astype(jnp.float32)
    grad_sum = grad_sum.astype(jnp.bfloat16)
    grad_down = grad_sum[None, :, :model_width]
    grad_up = grad_sum[None, :, model_width:]

    weight_pieces = relay_gather(frozen_value_weight, members, groups, me, dp_index)
    if weight_pieces and len(weight_pieces[0]) == 2:
        weight_pieces = [(source, 0, value) for source, value in weight_pieces]
    adapter_output = jnp.einsum(
        "znr,zrm->znm", low_rank_state, up_block, preferred_element_type=jnp.float32
    ).reshape(tok_rows, value_width)
    live_flat = live_rows.reshape(tok_rows, 1)
    masked_cot = (output_gradient * live_flat).astype(jnp.bfloat16)

    output_total = ADAPTER_SCALE * adapter_output
    token_gradient = jnp.zeros((tok_rows, model_width), jnp.bfloat16)
    for source, chunk, weight_piece in weight_pieces:
        piece_rows = weight_piece.shape[0]
        column = source * shard_rows + chunk * piece_rows
        token_piece = lax.dynamic_slice_in_dim(tokens, column, piece_rows, axis=1)
        output_total = lax.optimization_barrier(output_total + jnp.dot(
            token_piece, weight_piece, preferred_element_type=jnp.float32
        ))
        down_piece = lax.dynamic_slice_in_dim(down_block, column, piece_rows, axis=2)
        backward_piece = lax.dot_general(
            masked_cot, weight_piece, (((1,), (1,)), ((), ())), preferred_element_type=jnp.float32
        ) + jnp.einsum(
            "uio,uof->uif", low_rank_gradient, down_piece, preferred_element_type=jnp.float32
        ).reshape(tok_rows, piece_rows)
        token_gradient = lax.dynamic_update_slice_in_dim(
            token_gradient, backward_piece.astype(jnp.bfloat16), column, axis=1
        )
    output = (live_flat * output_total).astype(jnp.bfloat16)
    return (output, token_gradient, grad_down, grad_up)


def solution(mesh):
    placed = (
        P(("fsdp", "dp"), None),
        P(("fsdp", "dp"), None),
        P("fsdp", None),
        P(("fsdp", "dp"), None, None),
        P(("fsdp", "dp"), None, None),
        P(("fsdp", "dp")),
        P(("fsdp", "dp")),
        P(),
    )
    return jax.shard_map(
        on_device,
        mesh=mesh,
        in_specs=placed,
        out_specs=(
            P(("fsdp", "dp"), None),
            P(("fsdp", "dp"), None),
            P(("fsdp", "dp"), None, None),
            P(("fsdp", "dp"), None, None),
        ),
        check_vma=False,
    )
```

```python
import jax
import jax.numpy as jnp
from jax import lax
from jax.sharding import PartitionSpec as P

ADAPTER_SCALE = 2.0
WEIGHT_CHUNKS = 2


def xor_pairs(count, step):
    return [(src, src ^ step) for src in range(count)]


def relay_gather(shard, members, groups, me, dp_index):
    flat = members * groups
    parity = me % 2
    if members != 8 or groups % 2 != 0:
        parts = {0: shard}
        for step in range(2, members, 2):
            parts[step] = lax.ppermute(shard, "fsdp", xor_pairs(members, step))
        for step in range(0, members, 2):
            parts[step + 1] = lax.ppermute(parts[step], "fsdp", xor_pairs(members, 1))
        return [(me ^ step, parts[step]) for step in range(members)]

    def flat_pairs(target):
        pairs = []
        for i in range(members):
            for d in range(groups):
                role = (i % 2) ^ (d % 2)
                ti, td = target(i, d, role)
                pairs.append((i * groups + d, ti * groups + td))
        return pairs

    first_pairs = flat_pairs(lambda i, d, role: (i ^ (2 + 2 * role), d))
    relay_pairs = flat_pairs(lambda i, d, role: (i ^ (4 - 2 * role), d))
    partner_pairs = flat_pairs(lambda i, d, role: (i, d ^ 1))
    role = parity ^ (dp_index % 2)
    sibling = me ^ 1
    sibling_role = 1 - role
    sources = [me, me ^ (2 + 2 * role), me ^ 6, me ^ (4 - 2 * role)]
    sibling_sources = [sibling, sibling ^ (2 + 2 * sibling_role), sibling ^ 6,
                       sibling ^ (4 - 2 * sibling_role)]
    rows = shard.shape[0] // WEIGHT_CHUNKS
    result = []
    previous = None
    offloaded = lax.all_gather(shard[rows:], "fsdp", axis=0, tiled=False)
    for member in range(members):
        result.append((4.0, member, 1, offloaded[member]))
    for k in range(WEIGHT_CHUNKS - 1):
        piece = shard[k * rows:(k + 1) * rows]
        result.append((0.0, sources[0], k, piece))
        result.append((1.0, sibling_sources[0], k, lax.ppermute(piece, "fsdp", xor_pairs(members, 1))))
        if previous is not None:
            piece, _ = lax.optimization_barrier((piece, previous))
        first = lax.ppermute(piece, ("fsdp", "dp"), first_pairs)
        previous = first
        result.append((2.0 + 2 * k, sources[1], k, first))
        result.append((3.0 + 2 * k, sibling_sources[1], k, lax.ppermute(first, "fsdp", xor_pairs(members, 1))))
        relayed = lax.ppermute(first, ("fsdp", "dp"), relay_pairs)
        partner = lax.ppermute(first, ("fsdp", "dp"), partner_pairs)
        result.append((4.5 + 2 * k, sources[2], k, relayed))
        result.append((4.5 + 2 * k, sources[3], k, partner))
        late = lax.ppermute(jnp.stack([relayed, partner]), "fsdp", xor_pairs(members, 1))
        result.append((5.5 + 2 * k, sibling_sources[2], k, late[0]))
        result.append((5.5 + 2 * k, sibling_sources[3], k, late[1]))
    result.sort(key=lambda item: item[0])
    return [item[1:] for item in result]


def on_device(
    tokens,
    output_gradient,
    frozen_value_weight,
    adapter_down_maps,
    adapter_up_maps,
    block_tenant_ids,
    block_live_rows,
    tenant_owner_slot,
):
    tok_rows, model_width = tokens.shape
    value_width = output_gradient.shape[1]
    blocks = block_tenant_ids.shape[0]
    block_length = tok_rows // blocks
    groups = lax.axis_size("dp")
    members = lax.axis_size("fsdp")
    shard_rows = frozen_value_weight.shape[0]
    me = lax.axis_index("fsdp")
    dp_index = lax.axis_index("dp")
    even_steps = list(range(2, members, 2))

    own_adapter = jnp.concatenate([adapter_down_maps[0], adapter_up_maps[0]], axis=1)
    by_step = {0: own_adapter}
    for step in even_steps:
        by_step[step] = lax.ppermute(own_adapter, "fsdp", xor_pairs(members, step))
    same_parity = jnp.stack([by_step[step] for step in range(0, members, 2)])
    other_parity = lax.ppermute(same_parity, "fsdp", xor_pairs(members, 1))
    for index, step in enumerate(range(0, members, 2)):
        by_step[step ^ 1] = other_parity[index]
    adapter_stack = jnp.stack([by_step[step] for step in range(members)])

    slot_ids = jnp.take(tenant_owner_slot, block_tenant_ids)
    member_ids = slot_ids // groups
    picked = jnp.stack([lax.dynamic_index_in_dim(adapter_stack, me ^ member_ids[b], 0, keepdims=False)
                        for b in range(blocks)])
    down_block = picked[:, :, :model_width]
    up_block = picked[:, :, model_width:]

    live_rows = (jnp.arange(block_length)[None, :] < block_live_rows[:, None]).astype(jnp.float32)
    live_column = live_rows[:, :, None]
    token_blocks = tokens.reshape(blocks, block_length, model_width)
    cot_blocks = output_gradient.reshape(blocks, block_length, value_width)

    low_rank_state = (
        jnp.einsum("cvj,coj->cvo", token_blocks, down_block, preferred_element_type=jnp.float32)
        * live_column
    ).astype(jnp.bfloat16)
    low_rank_gradient = (
        ADAPTER_SCALE
        * jnp.einsum("btv,bkv->btk", cot_blocks, up_block, preferred_element_type=jnp.float32)
        * live_column
    ).astype(jnp.bfloat16)

    partial_down = jnp.einsum(
        "vio,vih->voh", low_rank_gradient, token_blocks, preferred_element_type=jnp.float32
    )
    partial_up = ADAPTER_SCALE * jnp.einsum(
        "btk,btv->bkv", low_rank_state, cot_blocks, preferred_element_type=jnp.float32
    )
    partial = jnp.concatenate([partial_down, partial_up], axis=2)

    def table_row(member):
        row = jnp.zeros(partial.shape[1:], jnp.float32)
        for b in range(blocks):
            row = row + jnp.where(member_ids[b] == member, partial[b], 0.0)
        return row.astype(jnp.bfloat16)

    sibling = me ^ 1
    for_sibling = jnp.stack([table_row(sibling ^ step) for step in range(0, members, 2)])
    from_sibling = lax.ppermute(for_sibling, "fsdp", xor_pairs(members, 1))
    pair_sums = [
        table_row(me ^ step).astype(jnp.float32) + from_sibling[index].astype(jnp.float32)
        for index, step in enumerate(range(0, members, 2))
    ]
    grad_sum = pair_sums[0]
    for index, step in enumerate(even_steps):
        sent = pair_sums[index + 1].astype(jnp.bfloat16)
        grad_sum = grad_sum + lax.ppermute(sent, "fsdp", xor_pairs(members, step)).astype(jnp.float32)
    grad_sum = grad_sum.astype(jnp.bfloat16)
    grad_down = grad_sum[None, :, :model_width]
    grad_up = grad_sum[None, :, model_width:]

    weight_pieces = relay_gather(frozen_value_weight, members, groups, me, dp_index)
    if weight_pieces and len(weight_pieces[0]) == 2:
        weight_pieces = [(source, 0, value) for source, value in weight_pieces]
    adapter_output = jnp.einsum(
        "znr,zrm->znm", low_rank_state, up_block, preferred_element_type=jnp.float32
    ).reshape(tok_rows, value_width)
    live_flat = live_rows.reshape(tok_rows, 1)
    masked_cot = (output_gradient * live_flat).astype(jnp.bfloat16)

    output_total = ADAPTER_SCALE * adapter_output
    token_gradient = jnp.zeros((tok_rows, model_width), jnp.bfloat16)
    for source, chunk, weight_piece in weight_pieces:
        piece_rows = weight_piece.shape[0]
        column = source * shard_rows + chunk * piece_rows
        token_piece = lax.dynamic_slice_in_dim(tokens, column, piece_rows, axis=1)
        output_total = lax.optimization_barrier(output_total + jnp.dot(
            token_piece, weight_piece, preferred_element_type=jnp.float32
        ))
        down_piece = lax.dynamic_slice_in_dim(down_block, column, piece_rows, axis=2)
        backward_piece = lax.dot_general(
            masked_cot, weight_piece, (((1,), (1,)), ((), ())), preferred_element_type=jnp.float32
        ) + jnp.einsum(
            "uio,uof->uif", low_rank_gradient, down_piece, preferred_element_type=jnp.float32
        ).reshape(tok_rows, piece_rows)
        token_gradient = lax.dynamic_update_slice_in_dim(
            token_gradient, backward_piece.astype(jnp.bfloat16), column, axis=1
        )
    output = (live_flat * output_total).astype(jnp.bfloat16)
    return (output, token_gradient, grad_down, grad_up)


def solution(mesh):
    placed = (
        P(("fsdp", "dp"), None),
        P(("fsdp", "dp"), None),
        P("fsdp", None),
        P(("fsdp", "dp"), None, None),
        P(("fsdp", "dp"), None, None),
        P(("fsdp", "dp")),
        P(("fsdp", "dp")),
        P(),
    )
    return jax.shard_map(
        on_device,
        mesh=mesh,
        in_specs=placed,
        out_specs=(
            P(("fsdp", "dp"), None),
            P(("fsdp", "dp"), None),
            P(("fsdp", "dp"), None, None),
            P(("fsdp", "dp"), None, None),
        ),
        check_vma=False,
    )
```

```python
import jax
import jax.numpy as jnp
from jax import lax
from jax.sharding import PartitionSpec as P

ADAPTER_SCALE = 2.0
WEIGHT_CHUNKS = 4


def xor_pairs(count, step):
    return [(src, src ^ step) for src in range(count)]


def relay_gather(shard, members, groups, me, dp_index):
    flat = members * groups
    parity = me % 2
    if members != 8 or groups % 2 != 0:
        parts = {0: shard}
        for step in range(2, members, 2):
            parts[step] = lax.ppermute(shard, "fsdp", xor_pairs(members, step))
        for step in range(0, members, 2):
            parts[step + 1] = lax.ppermute(parts[step], "fsdp", xor_pairs(members, 1))
        return [(me ^ step, parts[step]) for step in range(members)]

    def flat_pairs(target):
        pairs = []
        for i in range(members):
            for d in range(groups):
                role = (i % 2) ^ (d % 2)
                ti, td = target(i, d, role)
                pairs.append((i * groups + d, ti * groups + td))
        return pairs

    first_pairs = flat_pairs(lambda i, d, role: (i ^ (2 + 2 * role), d))
    relay_pairs = flat_pairs(lambda i, d, role: (i ^ (4 - 2 * role), d))
    partner_pairs = flat_pairs(lambda i, d, role: (i, d ^ 1))
    role = parity ^ (dp_index % 2)
    sibling = me ^ 1
    sibling_role = 1 - role
    sources = [me, me ^ (2 + 2 * role), me ^ 6, me ^ (4 - 2 * role)]
    sibling_sources = [sibling, sibling ^ (2 + 2 * sibling_role), sibling ^ 6,
                       sibling ^ (4 - 2 * sibling_role)]
    rows = shard.shape[0] // WEIGHT_CHUNKS
    result = []
    previous = None
    for k in range(WEIGHT_CHUNKS):
        piece = shard[k * rows:(k + 1) * rows]
        result.append((0.0, sources[0], k, piece))
        result.append((1.0, sibling_sources[0], k, lax.ppermute(piece, "fsdp", xor_pairs(members, 1))))
        if previous is not None:
            piece, _ = lax.optimization_barrier((piece, previous))
        first = lax.ppermute(piece, ("fsdp", "dp"), first_pairs)
        previous = first
        result.append((2.0 + 2 * k, sources[1], k, first))
        result.append((3.0 + 2 * k, sibling_sources[1], k, lax.ppermute(first, "fsdp", xor_pairs(members, 1))))
        relayed = lax.ppermute(first, ("fsdp", "dp"), relay_pairs)
        partner = lax.ppermute(first, ("fsdp", "dp"), partner_pairs)
        result.append((4.5 + 2 * k, sources[2], k, relayed))
        result.append((4.5 + 2 * k, sources[3], k, partner))
        late = lax.ppermute(jnp.stack([relayed, partner]), "fsdp", xor_pairs(members, 1))
        result.append((5.5 + 2 * k, sibling_sources[2], k, late[0]))
        result.append((5.5 + 2 * k, sibling_sources[3], k, late[1]))
    result.sort(key=lambda item: item[0])
    return [item[1:] for item in result]


def on_device(
    tokens,
    output_gradient,
    frozen_value_weight,
    adapter_down_maps,
    adapter_up_maps,
    block_tenant_ids,
    block_live_rows,
    tenant_owner_slot,
):
    tok_rows, model_width = tokens.shape
    value_width = output_gradient.shape[1]
    blocks = block_tenant_ids.shape[0]
    block_length = tok_rows // blocks
    groups = lax.axis_size("dp")
    members = lax.axis_size("fsdp")
    shard_rows = frozen_value_weight.shape[0]
    me = lax.axis_index("fsdp")
    dp_index = lax.axis_index("dp")
    even_steps = list(range(2, members, 2))

    own_adapter = jnp.concatenate([adapter_down_maps[0], adapter_up_maps[0]], axis=1)
    by_step = {0: own_adapter}
    for step in even_steps:
        by_step[step] = lax.ppermute(own_adapter, "fsdp", xor_pairs(members, step))
    same_parity = jnp.stack([by_step[step] for step in range(0, members, 2)])
    other_parity = lax.ppermute(same_parity, "fsdp", xor_pairs(members, 1))
    for index, step in enumerate(range(0, members, 2)):
        by_step[step ^ 1] = other_parity[index]
    adapter_stack = jnp.stack([by_step[step] for step in range(members)])

    slot_ids = jnp.take(tenant_owner_slot, block_tenant_ids)
    member_ids = slot_ids // groups
    picked = jnp.stack([lax.dynamic_index_in_dim(adapter_stack, me ^ member_ids[b], 0, keepdims=False)
                        for b in range(blocks)])
    down_block = picked[:, :, :model_width]
    up_block = picked[:, :, model_width:]

    live_rows = (jnp.arange(block_length)[None, :] < block_live_rows[:, None]).astype(jnp.float32)
    live_column = live_rows[:, :, None]
    token_blocks = tokens.reshape(blocks, block_length, model_width)
    cot_blocks = output_gradient.reshape(blocks, block_length, value_width)

    low_rank_state = (
        jnp.einsum("cvj,coj->cvo", token_blocks, down_block, preferred_element_type=jnp.float32)
        * live_column
    ).astype(jnp.bfloat16)
    low_rank_gradient = (
        ADAPTER_SCALE
        * jnp.einsum("btv,bkv->btk", cot_blocks, up_block, preferred_element_type=jnp.float32)
        * live_column
    ).astype(jnp.bfloat16)

    partial_down = jnp.einsum(
        "vio,vih->voh", low_rank_gradient, token_blocks, preferred_element_type=jnp.float32
    )
    partial_up = ADAPTER_SCALE * jnp.einsum(
        "btk,btv->bkv", low_rank_state, cot_blocks, preferred_element_type=jnp.float32
    )
    partial = jnp.concatenate([partial_down, partial_up], axis=2)

    def table_row(member):
        row = jnp.zeros(partial.shape[1:], jnp.float32)
        for b in range(blocks):
            row = row + jnp.where(member_ids[b] == member, partial[b], 0.0)
        return row.astype(jnp.bfloat16)

    sibling = me ^ 1
    for_sibling = jnp.stack([table_row(sibling ^ step) for step in range(0, members, 2)])
    from_sibling = lax.ppermute(for_sibling, "fsdp", xor_pairs(members, 1))
    pair_sums = [
        table_row(me ^ step).astype(jnp.float32) + from_sibling[index].astype(jnp.float32)
        for index, step in enumerate(range(0, members, 2))
    ]
    grad_sum = pair_sums[0]
    for index, step in enumerate(even_steps):
        sent = pair_sums[index + 1].astype(jnp.bfloat16)
        grad_sum = grad_sum + lax.ppermute(sent, "fsdp", xor_pairs(members, step)).astype(jnp.float32)
    grad_sum = grad_sum.astype(jnp.bfloat16)
    grad_down = grad_sum[None, :, :model_width]
    grad_up = grad_sum[None, :, model_width:]

    weight_pieces = relay_gather(frozen_value_weight, members, groups, me, dp_index)
    if weight_pieces and len(weight_pieces[0]) == 2:
        weight_pieces = [(source, 0, value) for source, value in weight_pieces]
    adapter_output = jnp.einsum(
        "znr,zrm->znm", low_rank_state, up_block, preferred_element_type=jnp.float32
    ).reshape(tok_rows, value_width)
    live_flat = live_rows.reshape(tok_rows, 1)
    masked_cot = (output_gradient * live_flat).astype(jnp.bfloat16)

    output_total = ADAPTER_SCALE * adapter_output
    token_gradient = jnp.zeros((tok_rows, model_width), jnp.bfloat16)
    for source, chunk, weight_piece in weight_pieces:
        piece_rows = weight_piece.shape[0]
        column = source * shard_rows + chunk * piece_rows
        token_piece = lax.dynamic_slice_in_dim(tokens, column, piece_rows, axis=1)
        output_total = lax.optimization_barrier(output_total + jnp.dot(
            token_piece, weight_piece, preferred_element_type=jnp.float32
        ))
        down_piece = lax.dynamic_slice_in_dim(down_block, column, piece_rows, axis=2)
        backward_piece = lax.dot_general(
            masked_cot, weight_piece, (((1,), (1,)), ((), ())), preferred_element_type=jnp.float32
        ) + jnp.einsum(
            "uio,uof->uif", low_rank_gradient, down_piece, preferred_element_type=jnp.float32
        ).reshape(tok_rows, piece_rows)
        token_gradient = lax.dynamic_update_slice_in_dim(
            token_gradient, backward_piece.astype(jnp.bfloat16), column, axis=1
        )
    output = (live_flat * output_total).astype(jnp.bfloat16)
    return (output, token_gradient, grad_down, grad_up)


def solution(mesh):
    placed = (
        P(("fsdp", "dp"), None),
        P(("fsdp", "dp"), None),
        P("fsdp", None),
        P(("fsdp", "dp"), None, None),
        P(("fsdp", "dp"), None, None),
        P(("fsdp", "dp")),
        P(("fsdp", "dp")),
        P(),
    )
    return jax.shard_map(
        on_device,
        mesh=mesh,
        in_specs=placed,
        out_specs=(
            P(("fsdp", "dp"), None),
            P(("fsdp", "dp"), None),
            P(("fsdp", "dp"), None, None),
            P(("fsdp", "dp"), None, None),
        ),
        check_vma=False,
    )
```

```python
import jax
import jax.numpy as jnp
from jax import lax
from jax.sharding import PartitionSpec as P

ADAPTER_SCALE = 2.0
WEIGHT_CHUNKS = 2


def xor_pairs(count, step):
    return [(src, src ^ step) for src in range(count)]


def relay_gather(shard, members, groups, me, dp_index):
    flat = members * groups
    parity = me % 2
    if members != 8 or groups % 2 != 0:
        parts = {0: shard}
        for step in range(2, members, 2):
            parts[step] = lax.ppermute(shard, "fsdp", xor_pairs(members, step))
        for step in range(0, members, 2):
            parts[step + 1] = lax.ppermute(parts[step], "fsdp", xor_pairs(members, 1))
        return [(me ^ step, parts[step]) for step in range(members)]

    def flat_pairs(target):
        pairs = []
        for i in range(members):
            for d in range(groups):
                role = (i % 2) ^ (d % 2)
                ti, td = target(i, d, role)
                pairs.append((i * groups + d, ti * groups + td))
        return pairs

    first_pairs = flat_pairs(lambda i, d, role: (i ^ (2 + 2 * role), d))
    relay_pairs = flat_pairs(lambda i, d, role: (i ^ (4 - 2 * role), d))
    partner_pairs = flat_pairs(lambda i, d, role: (i, d ^ 1))
    role = parity ^ (dp_index % 2)
    sibling = me ^ 1
    sibling_role = 1 - role
    sources = [me, me ^ (2 + 2 * role), me ^ 6, me ^ (4 - 2 * role)]
    sibling_sources = [sibling, sibling ^ (2 + 2 * sibling_role), sibling ^ 6,
                       sibling ^ (4 - 2 * sibling_role)]
    rows = shard.shape[0] // WEIGHT_CHUNKS
    result = []
    previous = None
    for k in range(WEIGHT_CHUNKS):
        piece = shard[k * rows:(k + 1) * rows]
        result.append((0.0, sources[0], k, piece))
        result.append((1.0, sibling_sources[0], k, lax.ppermute(piece, "fsdp", xor_pairs(members, 1))))
        if previous is not None:
            piece, _ = lax.optimization_barrier((piece, previous))
        first = lax.ppermute(piece, ("fsdp", "dp"), first_pairs)
        previous = first
        result.append((2.0 + 2 * k, sources[1], k, first))
        result.append((3.0 + 2 * k, sibling_sources[1], k, lax.ppermute(first, "fsdp", xor_pairs(members, 1))))
        relayed = lax.ppermute(first, ("fsdp", "dp"), relay_pairs)
        partner = lax.ppermute(first, ("fsdp", "dp"), partner_pairs)
        result.append((4.5 + 2 * k, sources[2], k, relayed))
        result.append((4.5 + 2 * k, sources[3], k, partner))
        late = lax.ppermute(jnp.stack([relayed, partner]), "fsdp", xor_pairs(members, 1))
        result.append((5.5 + 2 * k, sibling_sources[2], k, late[0]))
        result.append((5.5 + 2 * k, sibling_sources[3], k, late[1]))
    result.sort(key=lambda item: item[0])
    return [item[1:] for item in result]


def on_device(
    tokens,
    output_gradient,
    frozen_value_weight,
    adapter_down_maps,
    adapter_up_maps,
    block_tenant_ids,
    block_live_rows,
    tenant_owner_slot,
):
    tok_rows, model_width = tokens.shape
    value_width = output_gradient.shape[1]
    blocks = block_tenant_ids.shape[0]
    block_length = tok_rows // blocks
    groups = lax.axis_size("dp")
    members = lax.axis_size("fsdp")
    shard_rows = frozen_value_weight.shape[0]
    me = lax.axis_index("fsdp")
    dp_index = lax.axis_index("dp")
    even_steps = list(range(2, members, 2))

    own_adapter = jnp.concatenate([adapter_down_maps[0], adapter_up_maps[0]], axis=1)
    by_step = {0: own_adapter}
    for step in even_steps:
        by_step[step] = lax.ppermute(own_adapter, "fsdp", xor_pairs(members, step))
    same_parity = jnp.stack([by_step[step] for step in range(0, members, 2)])
    other_parity = lax.ppermute(same_parity, "fsdp", xor_pairs(members, 1))
    for index, step in enumerate(range(0, members, 2)):
        by_step[step ^ 1] = other_parity[index]
    adapter_stack = jnp.stack([by_step[step] for step in range(members)])

    slot_ids = jnp.take(tenant_owner_slot, block_tenant_ids)
    member_ids = slot_ids // groups
    picked = jnp.stack([lax.dynamic_index_in_dim(adapter_stack, me ^ member_ids[b], 0, keepdims=False)
                        for b in range(blocks)])
    down_block = picked[:, :, :model_width]
    up_block = picked[:, :, model_width:]

    live_rows = (jnp.arange(block_length)[None, :] < block_live_rows[:, None]).astype(jnp.float32)
    live_column = live_rows[:, :, None]
    token_blocks = tokens.reshape(blocks, block_length, model_width)
    cot_blocks = output_gradient.reshape(blocks, block_length, value_width)

    low_rank_state = (
        jnp.einsum("cvj,coj->cvo", token_blocks, down_block, preferred_element_type=jnp.float32)
        * live_column
    ).astype(jnp.bfloat16)
    low_rank_gradient = (
        ADAPTER_SCALE
        * jnp.einsum("btv,bkv->btk", cot_blocks, up_block, preferred_element_type=jnp.float32)
        * live_column
    ).astype(jnp.bfloat16)

    partial_down = jnp.einsum(
        "vio,vih->voh", low_rank_gradient, token_blocks, preferred_element_type=jnp.float32
    )
    partial_up = ADAPTER_SCALE * jnp.einsum(
        "btk,btv->bkv", low_rank_state, cot_blocks, preferred_element_type=jnp.float32
    )
    partial = jnp.concatenate([partial_down, partial_up], axis=2)

    def table_row(member):
        row = jnp.zeros(partial.shape[1:], jnp.float32)
        for b in range(blocks):
            row = row + jnp.where(member_ids[b] == member, partial[b], 0.0)
        return row.astype(jnp.bfloat16)

    sibling = me ^ 1
    for_sibling = jnp.stack([table_row(sibling ^ step) for step in range(0, members, 2)])
    from_sibling = lax.ppermute(for_sibling, "fsdp", xor_pairs(members, 1))
    pair_sums = [
        table_row(me ^ step).astype(jnp.float32) + from_sibling[index].astype(jnp.float32)
        for index, step in enumerate(range(0, members, 2))
    ]
    weight_pieces = relay_gather(frozen_value_weight, members, groups, me, dp_index)
    if weight_pieces and len(weight_pieces[0]) == 2:
        weight_pieces = [(source, 0, value) for source, value in weight_pieces]
    last_pieces = tuple(value for _, _, value in weight_pieces[-4:])
    grad_sum = pair_sums[0]
    for index, step in enumerate(even_steps):
        sent = pair_sums[index + 1].astype(jnp.bfloat16)
        sent, _ = lax.optimization_barrier((sent, last_pieces))
        grad_sum = grad_sum + lax.ppermute(sent, "fsdp", xor_pairs(members, step)).astype(jnp.float32)
    grad_sum = grad_sum.astype(jnp.bfloat16)
    grad_down = grad_sum[None, :, :model_width]
    grad_up = grad_sum[None, :, model_width:]

    adapter_output = jnp.einsum(
        "znr,zrm->znm", low_rank_state, up_block, preferred_element_type=jnp.float32
    ).reshape(tok_rows, value_width)
    live_flat = live_rows.reshape(tok_rows, 1)
    masked_cot = (output_gradient * live_flat).astype(jnp.bfloat16)

    output_total = ADAPTER_SCALE * adapter_output
    token_gradient = jnp.zeros((tok_rows, model_width), jnp.bfloat16)
    for source, chunk, weight_piece in weight_pieces:
        piece_rows = weight_piece.shape[0]
        column = source * shard_rows + chunk * piece_rows
        token_piece = lax.dynamic_slice_in_dim(tokens, column, piece_rows, axis=1)
        output_total = lax.optimization_barrier(output_total + jnp.dot(
            token_piece, weight_piece, preferred_element_type=jnp.float32
        ))
        down_piece = lax.dynamic_slice_in_dim(down_block, column, piece_rows, axis=2)
        backward_piece = lax.dot_general(
            masked_cot, weight_piece, (((1,), (1,)), ((), ())), preferred_element_type=jnp.float32
        ) + jnp.einsum(
            "uio,uof->uif", low_rank_gradient, down_piece, preferred_element_type=jnp.float32
        ).reshape(tok_rows, piece_rows)
        token_gradient = lax.dynamic_update_slice_in_dim(
            token_gradient, backward_piece.astype(jnp.bfloat16), column, axis=1
        )
    output = (live_flat * output_total).astype(jnp.bfloat16)
    return (output, token_gradient, grad_down, grad_up)


def solution(mesh):
    placed = (
        P(("fsdp", "dp"), None),
        P(("fsdp", "dp"), None),
        P("fsdp", None),
        P(("fsdp", "dp"), None, None),
        P(("fsdp", "dp"), None, None),
        P(("fsdp", "dp")),
        P(("fsdp", "dp")),
        P(),
    )
    return jax.shard_map(
        on_device,
        mesh=mesh,
        in_specs=placed,
        out_specs=(
            P(("fsdp", "dp"), None),
            P(("fsdp", "dp"), None),
            P(("fsdp", "dp"), None, None),
            P(("fsdp", "dp"), None, None),
        ),
        check_vma=False,
    )
```

```python
import jax
import jax.numpy as jnp
from jax import lax
from jax.sharding import PartitionSpec as P

ADAPTER_SCALE = 2.0
WEIGHT_CHUNKS = 2


def xor_pairs(count, step):
    return [(src, src ^ step) for src in range(count)]


def relay_gather(shard, members, groups, me, dp_index):
    flat = members * groups
    parity = me % 2
    if members != 8 or groups % 2 != 0:
        parts = {0: shard}
        for step in range(2, members, 2):
            parts[step] = lax.ppermute(shard, "fsdp", xor_pairs(members, step))
        for step in range(0, members, 2):
            parts[step + 1] = lax.ppermute(parts[step], "fsdp", xor_pairs(members, 1))
        return [(me ^ step, parts[step]) for step in range(members)]

    def flat_pairs(target):
        pairs = []
        for i in range(members):
            for d in range(groups):
                role = (i % 2) ^ (d % 2)
                ti, td = target(i, d, role)
                pairs.append((i * groups + d, ti * groups + td))
        return pairs

    first_pairs = flat_pairs(lambda i, d, role: (i ^ (2 + 2 * role), d))
    relay_pairs = flat_pairs(lambda i, d, role: (i ^ (4 - 2 * role), d))
    partner_pairs = flat_pairs(lambda i, d, role: (i, d ^ 1))
    role = parity ^ (dp_index % 2)
    sibling = me ^ 1
    sibling_role = 1 - role
    sources = [me, me ^ (2 + 2 * role), me ^ 6, me ^ (4 - 2 * role)]
    sibling_sources = [sibling, sibling ^ (2 + 2 * sibling_role), sibling ^ 6,
                       sibling ^ (4 - 2 * sibling_role)]
    rows = shard.shape[0] // WEIGHT_CHUNKS
    result = []
    previous = None
    for k in range(WEIGHT_CHUNKS):
        piece = shard[k * rows:(k + 1) * rows]
        result.append((0.0, sources[0], k, piece))
        result.append((1.0, sibling_sources[0], k, lax.ppermute(piece, "fsdp", xor_pairs(members, 1))))
        if previous is not None:
            piece, _ = lax.optimization_barrier((piece, previous))
        first = lax.ppermute(piece, ("fsdp", "dp"), first_pairs)
        previous = first
        result.append((2.0 + 2 * k, sources[1], k, first))
        result.append((3.0 + 2 * k, sibling_sources[1], k, lax.ppermute(first, "fsdp", xor_pairs(members, 1))))
        relayed = lax.ppermute(first, ("fsdp", "dp"), relay_pairs)
        partner = lax.ppermute(first, ("fsdp", "dp"), partner_pairs)
        result.append((4.5 + 2 * k, sources[2], k, relayed))
        result.append((4.5 + 2 * k, sources[3], k, partner))
        late = lax.ppermute(jnp.stack([relayed, partner]), "fsdp", xor_pairs(members, 1))
        result.append((5.5 + 2 * k, sibling_sources[2], k, late[0]))
        result.append((5.5 + 2 * k, sibling_sources[3], k, late[1]))
    result.sort(key=lambda item: item[0])
    return [item[1:] for item in result]


def on_device(
    tokens,
    output_gradient,
    frozen_value_weight,
    adapter_down_maps,
    adapter_up_maps,
    block_tenant_ids,
    block_live_rows,
    tenant_owner_slot,
):
    tok_rows, model_width = tokens.shape
    value_width = output_gradient.shape[1]
    blocks = block_tenant_ids.shape[0]
    block_length = tok_rows // blocks
    groups = lax.axis_size("dp")
    members = lax.axis_size("fsdp")
    shard_rows = frozen_value_weight.shape[0]
    me = lax.axis_index("fsdp")
    dp_index = lax.axis_index("dp")
    even_steps = list(range(2, members, 2))

    own_adapter = jnp.concatenate([adapter_down_maps[0], adapter_up_maps[0]], axis=1)
    slot_ids = jnp.take(tenant_owner_slot, block_tenant_ids)
    member_ids = slot_ids // groups
    parity = me % 2
    doubling = members == 8
    if doubling:
        first_axis = 2 + 2 * parity
        second_axis = 6 - first_axis
        first_pairs = [(src, src ^ (2 + 2 * (src % 2))) for src in range(members)]
        second_pairs = [(src, src ^ (4 - 2 * (src % 2))) for src in range(members)]
        got_first = lax.ppermute(own_adapter, "fsdp", first_pairs)
        got_second = lax.ppermute(jnp.stack([own_adapter, got_first]), "fsdp", second_pairs)
        same_parity = jnp.stack([own_adapter, got_first, got_second[0], got_second[1]])
        same_members = [me, me ^ first_axis, me ^ second_axis, me ^ 6]
    else:
        same_list = [own_adapter] + [
            lax.ppermute(own_adapter, "fsdp", xor_pairs(members, step)) for step in even_steps
        ]
        same_parity = jnp.stack(same_list)
        same_members = [me ^ step for step in range(0, members, 2)]
    other_parity = lax.ppermute(same_parity, "fsdp", xor_pairs(members, 1))
    adapter_stack = jnp.concatenate([same_parity, other_parity])
    sibling_parity = 1 - parity
    if doubling:
        sibling_first = 2 + 2 * sibling_parity
        other_members = [me ^ 1, me ^ 1 ^ sibling_first, me ^ 1 ^ (6 - sibling_first), me ^ 7]
    else:
        other_members = [me ^ 1 ^ step for step in range(0, members, 2)]
    stack_members = jnp.stack([jnp.asarray(m, jnp.int32) for m in same_members + other_members])
    picked = jnp.stack([
        lax.dynamic_index_in_dim(
            adapter_stack, jnp.argmax(stack_members == member_ids[b]).astype(jnp.int32), 0,
            keepdims=False)
        for b in range(blocks)])
    down_block = picked[:, :, :model_width]
    up_block = picked[:, :, model_width:]

    live_rows = (jnp.arange(block_length)[None, :] < block_live_rows[:, None]).astype(jnp.float32)
    live_column = live_rows[:, :, None]
    token_blocks = tokens.reshape(blocks, block_length, model_width)
    cot_blocks = output_gradient.reshape(blocks, block_length, value_width)

    low_rank_state = (
        jnp.einsum("cvj,coj->cvo", token_blocks, down_block, preferred_element_type=jnp.float32)
        * live_column
    ).astype(jnp.bfloat16)
    low_rank_gradient = (
        ADAPTER_SCALE
        * jnp.einsum("btv,bkv->btk", cot_blocks, up_block, preferred_element_type=jnp.float32)
        * live_column
    ).astype(jnp.bfloat16)

    partial_down = jnp.einsum(
        "vio,vih->voh", low_rank_gradient, token_blocks, preferred_element_type=jnp.float32
    )
    partial_up = ADAPTER_SCALE * jnp.einsum(
        "btk,btv->bkv", low_rank_state, cot_blocks, preferred_element_type=jnp.float32
    )
    partial = jnp.concatenate([partial_down, partial_up], axis=2)

    def table_row(member):
        row = jnp.zeros(partial.shape[1:], jnp.float32)
        for b in range(blocks):
            row = row + jnp.where(member_ids[b] == member, partial[b], 0.0)
        return row.astype(jnp.bfloat16)

    sibling = me ^ 1
    for_sibling = jnp.stack([table_row(sibling ^ step) for step in range(0, members, 2)])
    from_sibling = lax.ppermute(for_sibling, "fsdp", xor_pairs(members, 1))
    pair_sums = [
        table_row(me ^ step).astype(jnp.float32) + from_sibling[index].astype(jnp.float32)
        for index, step in enumerate(range(0, members, 2))
    ]
    weight_pieces = relay_gather(frozen_value_weight, members, groups, me, dp_index)
    if weight_pieces and len(weight_pieces[0]) == 2:
        weight_pieces = [(source, 0, value) for source, value in weight_pieces]
    last_pieces = tuple(value for _, _, value in weight_pieces[-4:])
    if doubling:
        by_axis = jnp.stack(pair_sums)
        keep_first = lax.dynamic_index_in_dim(by_axis, second_axis // 2, 0, keepdims=False)
        send_first = jnp.stack([
            lax.dynamic_index_in_dim(by_axis, first_axis // 2, 0, keepdims=False), pair_sums[3]
        ]).astype(jnp.bfloat16)
        send_first, _ = lax.optimization_barrier((send_first, last_pieces))
        got = lax.ppermute(send_first, "fsdp", first_pairs).astype(jnp.float32)
        mine = pair_sums[0] + got[0]
        send_second = (keep_first + got[1]).astype(jnp.bfloat16)
        grad_sum = mine + lax.ppermute(send_second, "fsdp", second_pairs).astype(jnp.float32)
    else:
        grad_sum = pair_sums[0]
        for index, step in enumerate(even_steps):
            sent = pair_sums[index + 1].astype(jnp.bfloat16)
            sent, _ = lax.optimization_barrier((sent, last_pieces))
            grad_sum = grad_sum + lax.ppermute(sent, "fsdp", xor_pairs(members, step)).astype(jnp.float32)
    grad_sum = grad_sum.astype(jnp.bfloat16)
    grad_down = grad_sum[None, :, :model_width]
    grad_up = grad_sum[None, :, model_width:]

    adapter_output = jnp.einsum(
        "znr,zrm->znm", low_rank_state, up_block, preferred_element_type=jnp.float32
    ).reshape(tok_rows, value_width)
    live_flat = live_rows.reshape(tok_rows, 1)
    masked_cot = (output_gradient * live_flat).astype(jnp.bfloat16)

    output_total = ADAPTER_SCALE * adapter_output
    token_gradient = jnp.zeros((tok_rows, model_width), jnp.bfloat16)
    for source, chunk, weight_piece in weight_pieces:
        piece_rows = weight_piece.shape[0]
        column = source * shard_rows + chunk * piece_rows
        token_piece = lax.dynamic_slice_in_dim(tokens, column, piece_rows, axis=1)
        output_total = lax.optimization_barrier(output_total + jnp.dot(
            token_piece, weight_piece, preferred_element_type=jnp.float32
        ))
        down_piece = lax.dynamic_slice_in_dim(down_block, column, piece_rows, axis=2)
        backward_piece = lax.dot_general(
            masked_cot, weight_piece, (((1,), (1,)), ((), ())), preferred_element_type=jnp.float32
        ) + jnp.einsum(
            "uio,uof->uif", low_rank_gradient, down_piece, preferred_element_type=jnp.float32
        ).reshape(tok_rows, piece_rows)
        token_gradient = lax.dynamic_update_slice_in_dim(
            token_gradient, backward_piece.astype(jnp.bfloat16), column, axis=1
        )
    output = (live_flat * output_total).astype(jnp.bfloat16)
    return (output, token_gradient, grad_down, grad_up)


def solution(mesh):
    placed = (
        P(("fsdp", "dp"), None),
        P(("fsdp", "dp"), None),
        P("fsdp", None),
        P(("fsdp", "dp"), None, None),
        P(("fsdp", "dp"), None, None),
        P(("fsdp", "dp")),
        P(("fsdp", "dp")),
        P(),
    )
    return jax.shard_map(
        on_device,
        mesh=mesh,
        in_specs=placed,
        out_specs=(
            P(("fsdp", "dp"), None),
            P(("fsdp", "dp"), None),
            P(("fsdp", "dp"), None, None),
            P(("fsdp", "dp"), None, None),
        ),
        check_vma=False,
    )
```

```python
import jax
import jax.numpy as jnp
from jax import lax
from jax.sharding import PartitionSpec as P

ADAPTER_SCALE = 2.0
WEIGHT_CHUNKS = 2


def xor_pairs(count, step):
    return [(src, src ^ step) for src in range(count)]


def relay_gather(shard, members, groups, me, dp_index):
    flat = members * groups
    parity = me % 2
    if members != 8 or groups % 2 != 0:
        parts = {0: shard}
        for step in range(2, members, 2):
            parts[step] = lax.ppermute(shard, "fsdp", xor_pairs(members, step))
        for step in range(0, members, 2):
            parts[step + 1] = lax.ppermute(parts[step], "fsdp", xor_pairs(members, 1))
        return [(me ^ step, parts[step]) for step in range(members)]

    def flat_pairs(target):
        pairs = []
        for i in range(members):
            for d in range(groups):
                role = (i % 2) ^ (d % 2)
                ti, td = target(i, d, role)
                pairs.append((i * groups + d, ti * groups + td))
        return pairs

    first_pairs = flat_pairs(lambda i, d, role: (i ^ (2 + 2 * role), d))
    relay_pairs = flat_pairs(lambda i, d, role: (i ^ (4 - 2 * role), d))
    partner_pairs = flat_pairs(lambda i, d, role: (i, d ^ 1))
    role = parity ^ (dp_index % 2)
    sibling = me ^ 1
    sibling_role = 1 - role
    sources = [me, me ^ (2 + 2 * role), me ^ 6, me ^ (4 - 2 * role)]
    sibling_sources = [sibling, sibling ^ (2 + 2 * sibling_role), sibling ^ 6,
                       sibling ^ (4 - 2 * sibling_role)]
    rows = shard.shape[0] // WEIGHT_CHUNKS
    result = []
    previous = None
    for k in range(WEIGHT_CHUNKS):
        piece = shard[k * rows:(k + 1) * rows]
        result.append((0.0, sources[0], k, piece))
        result.append((1.0, sibling_sources[0], k, lax.ppermute(piece, "fsdp", xor_pairs(members, 1))))
        if previous is not None:
            piece, _ = lax.optimization_barrier((piece, previous))
        first = lax.ppermute(piece, ("fsdp", "dp"), first_pairs)
        previous = first
        result.append((2.0 + 2 * k, sources[1], k, first))
        result.append((3.0 + 2 * k, sibling_sources[1], k, lax.ppermute(first, "fsdp", xor_pairs(members, 1))))
        relayed = lax.ppermute(first, ("fsdp", "dp"), relay_pairs)
        partner = lax.ppermute(first, ("fsdp", "dp"), partner_pairs)
        result.append((4.5 + 2 * k, sources[2], k, relayed))
        result.append((4.5 + 2 * k, sources[3], k, partner))
        late = lax.ppermute(jnp.stack([relayed, partner]), "fsdp", xor_pairs(members, 1))
        result.append((5.5 + 2 * k, sibling_sources[2], k, late[0]))
        result.append((5.5 + 2 * k, sibling_sources[3], k, late[1]))
    result.sort(key=lambda item: item[0])
    return [item[1:] for item in result]


def on_device(
    tokens,
    output_gradient,
    frozen_value_weight,
    adapter_down_maps,
    adapter_up_maps,
    block_tenant_ids,
    block_live_rows,
    tenant_owner_slot,
):
    tok_rows, model_width = tokens.shape
    value_width = output_gradient.shape[1]
    blocks = block_tenant_ids.shape[0]
    block_length = tok_rows // blocks
    groups = lax.axis_size("dp")
    members = lax.axis_size("fsdp")
    shard_rows = frozen_value_weight.shape[0]
    me = lax.axis_index("fsdp")
    dp_index = lax.axis_index("dp")
    even_steps = list(range(2, members, 2))

    own_adapter = jnp.concatenate([adapter_down_maps[0], adapter_up_maps[0]], axis=1)
    by_step = {0: own_adapter}
    for step in even_steps:
        by_step[step] = lax.ppermute(own_adapter, "fsdp", xor_pairs(members, step))
    same_parity = jnp.stack([by_step[step] for step in range(0, members, 2)])
    other_parity = lax.ppermute(same_parity, "fsdp", xor_pairs(members, 1))
    for index, step in enumerate(range(0, members, 2)):
        by_step[step ^ 1] = other_parity[index]
    adapter_stack = jnp.stack([by_step[step] for step in range(members)])

    slot_ids = jnp.take(tenant_owner_slot, block_tenant_ids)
    member_ids = slot_ids // groups
    picked = jnp.stack([lax.dynamic_index_in_dim(adapter_stack, me ^ member_ids[b], 0, keepdims=False)
                        for b in range(blocks)])
    down_block = picked[:, :, :model_width]
    up_block = picked[:, :, model_width:]

    live_rows = (jnp.arange(block_length)[None, :] < block_live_rows[:, None]).astype(jnp.float32)
    live_column = live_rows[:, :, None]
    token_blocks = tokens.reshape(blocks, block_length, model_width)
    cot_blocks = output_gradient.reshape(blocks, block_length, value_width)

    low_rank_state = (
        jnp.einsum("cvj,coj->cvo", token_blocks, down_block, preferred_element_type=jnp.float32)
        * live_column
    ).astype(jnp.bfloat16)
    low_rank_gradient = (
        ADAPTER_SCALE
        * jnp.einsum("btv,bkv->btk", cot_blocks, up_block, preferred_element_type=jnp.float32)
        * live_column
    ).astype(jnp.bfloat16)

    partial_down = jnp.einsum(
        "vio,vih->voh", low_rank_gradient, token_blocks, preferred_element_type=jnp.float32
    )
    partial_up = ADAPTER_SCALE * jnp.einsum(
        "btk,btv->bkv", low_rank_state, cot_blocks, preferred_element_type=jnp.float32
    )
    partial = jnp.concatenate([partial_down, partial_up], axis=2)

    def table_row(member):
        row = jnp.zeros(partial.shape[1:], jnp.float32)
        for b in range(blocks):
            row = row + jnp.where(member_ids[b] == member, partial[b], 0.0)
        return row.astype(jnp.bfloat16)

    sibling = me ^ 1
    for_sibling = jnp.stack([table_row(sibling ^ step) for step in range(0, members, 2)])
    from_sibling = lax.ppermute(for_sibling, "fsdp", xor_pairs(members, 1))
    pair_sums = [
        table_row(me ^ step).astype(jnp.float32) + from_sibling[index].astype(jnp.float32)
        for index, step in enumerate(range(0, members, 2))
    ]
    weight_pieces = relay_gather(frozen_value_weight, members, groups, me, dp_index)
    if weight_pieces and len(weight_pieces[0]) == 2:
        weight_pieces = [(source, 0, value) for source, value in weight_pieces]
    last_pieces = tuple(value for _, _, value in weight_pieces[-4:-2])
    grad_sum = pair_sums[0]
    for index, step in enumerate(even_steps):
        sent = pair_sums[index + 1].astype(jnp.bfloat16)
        sent, _ = lax.optimization_barrier((sent, last_pieces))
        grad_sum = grad_sum + lax.ppermute(sent, "fsdp", xor_pairs(members, step)).astype(jnp.float32)
    grad_sum = grad_sum.astype(jnp.bfloat16)
    grad_down = grad_sum[None, :, :model_width]
    grad_up = grad_sum[None, :, model_width:]

    adapter_output = jnp.einsum(
        "znr,zrm->znm", low_rank_state, up_block, preferred_element_type=jnp.float32
    ).reshape(tok_rows, value_width)
    live_flat = live_rows.reshape(tok_rows, 1)
    masked_cot = (output_gradient * live_flat).astype(jnp.bfloat16)

    output_total = ADAPTER_SCALE * adapter_output
    token_gradient = jnp.zeros((tok_rows, model_width), jnp.bfloat16)
    for source, chunk, weight_piece in weight_pieces:
        piece_rows = weight_piece.shape[0]
        column = source * shard_rows + chunk * piece_rows
        token_piece = lax.dynamic_slice_in_dim(tokens, column, piece_rows, axis=1)
        output_total = lax.optimization_barrier(output_total + jnp.dot(
            token_piece, weight_piece, preferred_element_type=jnp.float32
        ))
        down_piece = lax.dynamic_slice_in_dim(down_block, column, piece_rows, axis=2)
        backward_piece = lax.dot_general(
            masked_cot, weight_piece, (((1,), (1,)), ((), ())), preferred_element_type=jnp.float32
        ) + jnp.einsum(
            "uio,uof->uif", low_rank_gradient, down_piece, preferred_element_type=jnp.float32
        ).reshape(tok_rows, piece_rows)
        token_gradient = lax.dynamic_update_slice_in_dim(
            token_gradient, backward_piece.astype(jnp.bfloat16), column, axis=1
        )
    output = (live_flat * output_total).astype(jnp.bfloat16)
    return (output, token_gradient, grad_down, grad_up)


def solution(mesh):
    placed = (
        P(("fsdp", "dp"), None),
        P(("fsdp", "dp"), None),
        P("fsdp", None),
        P(("fsdp", "dp"), None, None),
        P(("fsdp", "dp"), None, None),
        P(("fsdp", "dp")),
        P(("fsdp", "dp")),
        P(),
    )
    return jax.shard_map(
        on_device,
        mesh=mesh,
        in_specs=placed,
        out_specs=(
            P(("fsdp", "dp"), None),
            P(("fsdp", "dp"), None),
            P(("fsdp", "dp"), None, None),
            P(("fsdp", "dp"), None, None),
        ),
        check_vma=False,
    )
```

```python
import jax
import jax.numpy as jnp
from jax import lax
from jax.sharding import PartitionSpec as P

ADAPTER_SCALE = 2.0


def xor_pairs(count, step):
    return [(src, src ^ step) for src in range(count)]


def relay_gather(shard, members, groups, me, dp_index):
    flat = members * groups
    parity = me % 2
    if members != 8 or groups % 2 != 0:
        parts = {0: shard}
        for step in range(2, members, 2):
            parts[step] = lax.ppermute(shard, "fsdp", xor_pairs(members, step))
        for step in range(0, members, 2):
            parts[step + 1] = lax.ppermute(parts[step], "fsdp", xor_pairs(members, 1))
        return [(me ^ step, parts[step]) for step in range(members)]

    def flat_pairs(target):
        pairs = []
        for i in range(members):
            for d in range(groups):
                role = (i % 2) ^ (d % 2)
                ti, td = target(i, d, role)
                pairs.append((i * groups + d, ti * groups + td))
        return pairs

    first_pairs = flat_pairs(lambda i, d, role: (i ^ (2 + 2 * role), d))
    relay_pairs = flat_pairs(lambda i, d, role: (i ^ (4 - 2 * role), d))
    partner_pairs = flat_pairs(lambda i, d, role: (i, d ^ 1))
    role = parity ^ (dp_index % 2)
    sibling = me ^ 1
    sibling_role = 1 - role
    sources = [me, me ^ (2 + 2 * role), me ^ 6, me ^ (4 - 2 * role)]
    sibling_sources = [sibling, sibling ^ (2 + 2 * sibling_role), sibling ^ 6,
                       sibling ^ (4 - 2 * sibling_role)]
    bounds = [0, shard.shape[0] // 4, shard.shape[0]]
    result = []
    previous = None
    for k in range(len(bounds) - 1):
        piece = shard[bounds[k]:bounds[k + 1]]
        result.append((0.0, sources[0], bounds[k], piece))
        result.append((1.0, sibling_sources[0], bounds[k], lax.ppermute(piece, "fsdp", xor_pairs(members, 1))))
        if previous is not None:
            piece, _ = lax.optimization_barrier((piece, previous))
        first = lax.ppermute(piece, ("fsdp", "dp"), first_pairs)
        previous = first
        result.append((2.0 + 2 * k, sources[1], bounds[k], first))
        result.append((3.0 + 2 * k, sibling_sources[1], bounds[k], lax.ppermute(first, "fsdp", xor_pairs(members, 1))))
        relayed = lax.ppermute(first, ("fsdp", "dp"), relay_pairs)
        partner = lax.ppermute(first, ("fsdp", "dp"), partner_pairs)
        result.append((4.5 + 2 * k, sources[2], bounds[k], relayed))
        result.append((4.5 + 2 * k, sources[3], bounds[k], partner))
        late = lax.ppermute(jnp.stack([relayed, partner]), "fsdp", xor_pairs(members, 1))
        result.append((5.5 + 2 * k, sibling_sources[2], bounds[k], late[0]))
        result.append((5.5 + 2 * k, sibling_sources[3], bounds[k], late[1]))
    result.sort(key=lambda item: item[0])
    return [item[1:] for item in result]


def on_device(
    tokens,
    output_gradient,
    frozen_value_weight,
    adapter_down_maps,
    adapter_up_maps,
    block_tenant_ids,
    block_live_rows,
    tenant_owner_slot,
):
    tok_rows, model_width = tokens.shape
    value_width = output_gradient.shape[1]
    blocks = block_tenant_ids.shape[0]
    block_length = tok_rows // blocks
    groups = lax.axis_size("dp")
    members = lax.axis_size("fsdp")
    shard_rows = frozen_value_weight.shape[0]
    me = lax.axis_index("fsdp")
    dp_index = lax.axis_index("dp")
    even_steps = list(range(2, members, 2))

    own_adapter = jnp.concatenate([adapter_down_maps[0], adapter_up_maps[0]], axis=1)
    by_step = {0: own_adapter}
    for step in even_steps:
        by_step[step] = lax.ppermute(own_adapter, "fsdp", xor_pairs(members, step))
    same_parity = jnp.stack([by_step[step] for step in range(0, members, 2)])
    other_parity = lax.ppermute(same_parity, "fsdp", xor_pairs(members, 1))
    for index, step in enumerate(range(0, members, 2)):
        by_step[step ^ 1] = other_parity[index]
    adapter_stack = jnp.stack([by_step[step] for step in range(members)])

    slot_ids = jnp.take(tenant_owner_slot, block_tenant_ids)
    member_ids = slot_ids // groups
    picked = jnp.stack([lax.dynamic_index_in_dim(adapter_stack, me ^ member_ids[b], 0, keepdims=False)
                        for b in range(blocks)])
    down_block = picked[:, :, :model_width]
    up_block = picked[:, :, model_width:]

    live_rows = (jnp.arange(block_length)[None, :] < block_live_rows[:, None]).astype(jnp.float32)
    live_column = live_rows[:, :, None]
    token_blocks = tokens.reshape(blocks, block_length, model_width)
    cot_blocks = output_gradient.reshape(blocks, block_length, value_width)

    low_rank_state = (
        jnp.einsum("cvj,coj->cvo", token_blocks, down_block, preferred_element_type=jnp.float32)
        * live_column
    ).astype(jnp.bfloat16)
    low_rank_gradient = (
        ADAPTER_SCALE
        * jnp.einsum("btv,bkv->btk", cot_blocks, up_block, preferred_element_type=jnp.float32)
        * live_column
    ).astype(jnp.bfloat16)

    partial_down = jnp.einsum(
        "vio,vih->voh", low_rank_gradient, token_blocks, preferred_element_type=jnp.float32
    )
    partial_up = ADAPTER_SCALE * jnp.einsum(
        "btk,btv->bkv", low_rank_state, cot_blocks, preferred_element_type=jnp.float32
    )
    partial = jnp.concatenate([partial_down, partial_up], axis=2)

    def table_row(member):
        row = jnp.zeros(partial.shape[1:], jnp.float32)
        for b in range(blocks):
            row = row + jnp.where(member_ids[b] == member, partial[b], 0.0)
        return row.astype(jnp.bfloat16)

    sibling = me ^ 1
    for_sibling = jnp.stack([table_row(sibling ^ step) for step in range(0, members, 2)])
    from_sibling = lax.ppermute(for_sibling, "fsdp", xor_pairs(members, 1))
    pair_sums = [
        table_row(me ^ step).astype(jnp.float32) + from_sibling[index].astype(jnp.float32)
        for index, step in enumerate(range(0, members, 2))
    ]
    weight_pieces = relay_gather(frozen_value_weight, members, groups, me, dp_index)
    if weight_pieces and len(weight_pieces[0]) == 2:
        weight_pieces = [(source, 0, value) for source, value in weight_pieces]
    last_pieces = tuple(value for _, _, value in weight_pieces[-4:])
    grad_sum = pair_sums[0]
    for index, step in enumerate(even_steps):
        sent = pair_sums[index + 1].astype(jnp.bfloat16)
        sent, _ = lax.optimization_barrier((sent, last_pieces))
        grad_sum = grad_sum + lax.ppermute(sent, "fsdp", xor_pairs(members, step)).astype(jnp.float32)
    grad_sum = grad_sum.astype(jnp.bfloat16)
    grad_down = grad_sum[None, :, :model_width]
    grad_up = grad_sum[None, :, model_width:]

    adapter_output = jnp.einsum(
        "znr,zrm->znm", low_rank_state, up_block, preferred_element_type=jnp.float32
    ).reshape(tok_rows, value_width)
    live_flat = live_rows.reshape(tok_rows, 1)
    masked_cot = (output_gradient * live_flat).astype(jnp.bfloat16)

    output_total = ADAPTER_SCALE * adapter_output
    token_gradient = jnp.zeros((tok_rows, model_width), jnp.bfloat16)
    for source, chunk, weight_piece in weight_pieces:
        piece_rows = weight_piece.shape[0]
        column = source * shard_rows + chunk
        token_piece = lax.dynamic_slice_in_dim(tokens, column, piece_rows, axis=1)
        output_total = lax.optimization_barrier(output_total + jnp.dot(
            token_piece, weight_piece, preferred_element_type=jnp.float32
        ))
        down_piece = lax.dynamic_slice_in_dim(down_block, column, piece_rows, axis=2)
        backward_piece = lax.dot_general(
            masked_cot, weight_piece, (((1,), (1,)), ((), ())), preferred_element_type=jnp.float32
        ) + jnp.einsum(
            "uio,uof->uif", low_rank_gradient, down_piece, preferred_element_type=jnp.float32
        ).reshape(tok_rows, piece_rows)
        token_gradient = lax.dynamic_update_slice_in_dim(
            token_gradient, backward_piece.astype(jnp.bfloat16), column, axis=1
        )
    output = (live_flat * output_total).astype(jnp.bfloat16)
    return (output, token_gradient, grad_down, grad_up)


def solution(mesh):
    placed = (
        P(("fsdp", "dp"), None),
        P(("fsdp", "dp"), None),
        P("fsdp", None),
        P(("fsdp", "dp"), None, None),
        P(("fsdp", "dp"), None, None),
        P(("fsdp", "dp")),
        P(("fsdp", "dp")),
        P(),
    )
    return jax.shard_map(
        on_device,
        mesh=mesh,
        in_specs=placed,
        out_specs=(
            P(("fsdp", "dp"), None),
            P(("fsdp", "dp"), None),
            P(("fsdp", "dp"), None, None),
            P(("fsdp", "dp"), None, None),
        ),
        check_vma=False,
    )
```

```python
import jax
import jax.numpy as jnp
from jax import lax
from jax.sharding import PartitionSpec as P

ADAPTER_SCALE = 2.0
WEIGHT_CHUNKS = 2


def xor_pairs(count, step):
    return [(src, src ^ step) for src in range(count)]


def relay_gather(shard, members, groups, me, dp_index):
    flat = members * groups
    parity = me % 2
    if members != 8 or groups % 2 != 0:
        parts = {0: shard}
        for step in range(2, members, 2):
            parts[step] = lax.ppermute(shard, "fsdp", xor_pairs(members, step))
        for step in range(0, members, 2):
            parts[step + 1] = lax.ppermute(parts[step], "fsdp", xor_pairs(members, 1))
        return [(me ^ step, parts[step]) for step in range(members)]

    def flat_pairs(target):
        pairs = []
        for i in range(members):
            for d in range(groups):
                role = (i % 2) ^ (d % 2)
                ti, td = target(i, d, role)
                pairs.append((i * groups + d, ti * groups + td))
        return pairs

    first_pairs = flat_pairs(lambda i, d, role: (i ^ (2 + 2 * role), d))
    relay_pairs = flat_pairs(lambda i, d, role: (i ^ (4 - 2 * role), d))
    partner_pairs = flat_pairs(lambda i, d, role: (i, d ^ 1))
    role = parity ^ (dp_index % 2)
    sibling = me ^ 1
    sibling_role = 1 - role
    sources = [me, me ^ (2 + 2 * role), me ^ 6, me ^ (4 - 2 * role)]
    sibling_sources = [sibling, sibling ^ (2 + 2 * sibling_role), sibling ^ 6,
                       sibling ^ (4 - 2 * sibling_role)]
    rows = shard.shape[0] // WEIGHT_CHUNKS
    result = []
    previous = None
    for k in range(WEIGHT_CHUNKS):
        piece = shard[k * rows:(k + 1) * rows]
        result.append((0.0, sources[0], k, piece))
        result.append((1.0, sibling_sources[0], k, lax.ppermute(piece, "fsdp", xor_pairs(members, 1))))
        if previous is not None:
            piece, _ = lax.optimization_barrier((piece, previous))
        first = lax.ppermute(piece, ("fsdp", "dp"), first_pairs)
        previous = first
        result.append((2.0 + 2 * k, sources[1], k, first))
        result.append((3.0 + 2 * k, sibling_sources[1], k, lax.ppermute(first, "fsdp", xor_pairs(members, 1))))
        relayed = lax.ppermute(first, ("fsdp", "dp"), relay_pairs)
        partner = lax.ppermute(first, ("fsdp", "dp"), partner_pairs)
        result.append((4.5 + 2 * k, sources[2], k, relayed))
        result.append((4.5 + 2 * k, sources[3], k, partner))
        late = lax.ppermute(jnp.stack([relayed, partner]), "fsdp", xor_pairs(members, 1))
        result.append((5.5 + 2 * k, sibling_sources[2], k, late[0]))
        result.append((5.5 + 2 * k, sibling_sources[3], k, late[1]))
    result.sort(key=lambda item: item[0])
    return [item[1:] for item in result]


def on_device(
    tokens,
    output_gradient,
    frozen_value_weight,
    adapter_down_maps,
    adapter_up_maps,
    block_tenant_ids,
    block_live_rows,
    tenant_owner_slot,
):
    tok_rows, model_width = tokens.shape
    value_width = output_gradient.shape[1]
    blocks = block_tenant_ids.shape[0]
    block_length = tok_rows // blocks
    groups = lax.axis_size("dp")
    members = lax.axis_size("fsdp")
    shard_rows = frozen_value_weight.shape[0]
    me = lax.axis_index("fsdp")
    dp_index = lax.axis_index("dp")
    even_steps = list(range(2, members, 2))

    weight_pieces = relay_gather(frozen_value_weight, members, groups, me, dp_index)
    if weight_pieces and len(weight_pieces[0]) == 2:
        weight_pieces = [(source, 0, value) for source, value in weight_pieces]

    own_adapter = jnp.concatenate([adapter_down_maps[0], adapter_up_maps[0]], axis=1)
    own_adapter, _ = lax.optimization_barrier((own_adapter, weight_pieces[4][2]))
    by_step = {0: own_adapter}
    for step in even_steps:
        by_step[step] = lax.ppermute(own_adapter, "fsdp", xor_pairs(members, step))
    same_parity = jnp.stack([by_step[step] for step in range(0, members, 2)])
    other_parity = lax.ppermute(same_parity, "fsdp", xor_pairs(members, 1))
    for index, step in enumerate(range(0, members, 2)):
        by_step[step ^ 1] = other_parity[index]
    adapter_stack = jnp.stack([by_step[step] for step in range(members)])

    slot_ids = jnp.take(tenant_owner_slot, block_tenant_ids)
    member_ids = slot_ids // groups
    picked = jnp.stack([lax.dynamic_index_in_dim(adapter_stack, me ^ member_ids[b], 0, keepdims=False)
                        for b in range(blocks)])
    down_block = picked[:, :, :model_width]
    up_block = picked[:, :, model_width:]

    live_rows = (jnp.arange(block_length)[None, :] < block_live_rows[:, None]).astype(jnp.float32)
    live_column = live_rows[:, :, None]
    token_blocks = tokens.reshape(blocks, block_length, model_width)
    cot_blocks = output_gradient.reshape(blocks, block_length, value_width)

    low_rank_state = (
        jnp.einsum("cvj,coj->cvo", token_blocks, down_block, preferred_element_type=jnp.float32)
        * live_column
    ).astype(jnp.bfloat16)
    low_rank_gradient = (
        ADAPTER_SCALE
        * jnp.einsum("btv,bkv->btk", cot_blocks, up_block, preferred_element_type=jnp.float32)
        * live_column
    ).astype(jnp.bfloat16)

    partial_down = jnp.einsum(
        "vio,vih->voh", low_rank_gradient, token_blocks, preferred_element_type=jnp.float32
    )
    partial_up = ADAPTER_SCALE * jnp.einsum(
        "btk,btv->bkv", low_rank_state, cot_blocks, preferred_element_type=jnp.float32
    )
    partial = jnp.concatenate([partial_down, partial_up], axis=2)

    def table_row(member):
        row = jnp.zeros(partial.shape[1:], jnp.float32)
        for b in range(blocks):
            row = row + jnp.where(member_ids[b] == member, partial[b], 0.0)
        return row.astype(jnp.bfloat16)

    sibling = me ^ 1
    for_sibling = jnp.stack([table_row(sibling ^ step) for step in range(0, members, 2)])
    from_sibling = lax.ppermute(for_sibling, "fsdp", xor_pairs(members, 1))
    pair_sums = [
        table_row(me ^ step).astype(jnp.float32) + from_sibling[index].astype(jnp.float32)
        for index, step in enumerate(range(0, members, 2))
    ]
    last_pieces = tuple(value for _, _, value in weight_pieces[-4:])
    grad_sum = pair_sums[0]
    for index, step in enumerate(even_steps):
        sent = pair_sums[index + 1].astype(jnp.bfloat16)
        sent, _ = lax.optimization_barrier((sent, last_pieces))
        grad_sum = grad_sum + lax.ppermute(sent, "fsdp", xor_pairs(members, step)).astype(jnp.float32)
    grad_sum = grad_sum.astype(jnp.bfloat16)
    grad_down = grad_sum[None, :, :model_width]
    grad_up = grad_sum[None, :, model_width:]

    adapter_output = jnp.einsum(
        "znr,zrm->znm", low_rank_state, up_block, preferred_element_type=jnp.float32
    ).reshape(tok_rows, value_width)
    live_flat = live_rows.reshape(tok_rows, 1)
    masked_cot = (output_gradient * live_flat).astype(jnp.bfloat16)

    output_total = ADAPTER_SCALE * adapter_output
    token_gradient = jnp.zeros((tok_rows, model_width), jnp.bfloat16)
    for source, chunk, weight_piece in weight_pieces:
        piece_rows = weight_piece.shape[0]
        column = source * shard_rows + chunk * piece_rows
        token_piece = lax.dynamic_slice_in_dim(tokens, column, piece_rows, axis=1)
        output_total = lax.optimization_barrier(output_total + jnp.dot(
            token_piece, weight_piece, preferred_element_type=jnp.float32
        ))
        down_piece = lax.dynamic_slice_in_dim(down_block, column, piece_rows, axis=2)
        backward_piece = lax.dot_general(
            masked_cot, weight_piece, (((1,), (1,)), ((), ())), preferred_element_type=jnp.float32
        ) + jnp.einsum(
            "uio,uof->uif", low_rank_gradient, down_piece, preferred_element_type=jnp.float32
        ).reshape(tok_rows, piece_rows)
        token_gradient = lax.dynamic_update_slice_in_dim(
            token_gradient, backward_piece.astype(jnp.bfloat16), column, axis=1
        )
    output = (live_flat * output_total).astype(jnp.bfloat16)
    return (output, token_gradient, grad_down, grad_up)


def solution(mesh):
    placed = (
        P(("fsdp", "dp"), None),
        P(("fsdp", "dp"), None),
        P("fsdp", None),
        P(("fsdp", "dp"), None, None),
        P(("fsdp", "dp"), None, None),
        P(("fsdp", "dp")),
        P(("fsdp", "dp")),
        P(),
    )
    return jax.shard_map(
        on_device,
        mesh=mesh,
        in_specs=placed,
        out_specs=(
            P(("fsdp", "dp"), None),
            P(("fsdp", "dp"), None),
            P(("fsdp", "dp"), None, None),
            P(("fsdp", "dp"), None, None),
        ),
        check_vma=False,
    )
```

```python
import jax
import jax.numpy as jnp
from jax import lax
from jax.sharding import PartitionSpec as P

ADAPTER_SCALE = 2.0
WEIGHT_CHUNKS = 2


def xor_pairs(count, step):
    return [(src, src ^ step) for src in range(count)]


def relay_gather(shard, members, groups, me, dp_index):
    flat = members * groups
    parity = me % 2
    if members != 8 or groups % 2 != 0:
        parts = {0: shard}
        for step in range(2, members, 2):
            parts[step] = lax.ppermute(shard, "fsdp", xor_pairs(members, step))
        for step in range(0, members, 2):
            parts[step + 1] = lax.ppermute(parts[step], "fsdp", xor_pairs(members, 1))
        return [(me ^ step, parts[step]) for step in range(members)]

    def flat_pairs(target):
        pairs = []
        for i in range(members):
            for d in range(groups):
                role = (i % 2) ^ (d % 2)
                ti, td = target(i, d, role)
                pairs.append((i * groups + d, ti * groups + td))
        return pairs

    first_pairs = flat_pairs(lambda i, d, role: (i ^ (2 + 2 * role), d))
    relay_pairs = flat_pairs(lambda i, d, role: (i ^ (4 - 2 * role), d))
    partner_pairs = flat_pairs(lambda i, d, role: (i, d ^ 1))
    role = parity ^ (dp_index % 2)
    sibling = me ^ 1
    sibling_role = 1 - role
    sources = [me, me ^ (2 + 2 * role), me ^ 6, me ^ (4 - 2 * role)]
    sibling_sources = [sibling, sibling ^ (2 + 2 * sibling_role), sibling ^ 6,
                       sibling ^ (4 - 2 * sibling_role)]
    rows = shard.shape[0] // WEIGHT_CHUNKS
    result = []
    previous = None
    for k in range(WEIGHT_CHUNKS):
        piece = shard[k * rows:(k + 1) * rows]
        result.append((0.0, sources[0], k, piece))
        result.append((1.0, sibling_sources[0], k, lax.ppermute(piece, "fsdp", xor_pairs(members, 1))))
        if previous is not None:
            piece, _ = lax.optimization_barrier((piece, previous))
        first = lax.ppermute(piece, ("fsdp", "dp"), first_pairs)
        previous = first
        result.append((2.0 + 2 * k, sources[1], k, first))
        result.append((3.0 + 2 * k, sibling_sources[1], k, lax.ppermute(first, "fsdp", xor_pairs(members, 1))))
        relayed = lax.ppermute(first, ("fsdp", "dp"), relay_pairs)
        partner = lax.ppermute(first, ("fsdp", "dp"), partner_pairs)
        result.append((4.5 + 2 * k, sources[2], k, relayed))
        result.append((4.5 + 2 * k, sources[3], k, partner))
        late = lax.ppermute(jnp.stack([relayed, partner]), "fsdp", xor_pairs(members, 1))
        result.append((5.5 + 2 * k, sibling_sources[2], k, late[0]))
        result.append((5.5 + 2 * k, sibling_sources[3], k, late[1]))
    result.sort(key=lambda item: item[0])
    return [item[1:] for item in result]


def on_device(
    tokens,
    output_gradient,
    frozen_value_weight,
    adapter_down_maps,
    adapter_up_maps,
    block_tenant_ids,
    block_live_rows,
    tenant_owner_slot,
):
    tok_rows, model_width = tokens.shape
    value_width = output_gradient.shape[1]
    blocks = block_tenant_ids.shape[0]
    block_length = tok_rows // blocks
    groups = lax.axis_size("dp")
    members = lax.axis_size("fsdp")
    shard_rows = frozen_value_weight.shape[0]
    me = lax.axis_index("fsdp")
    dp_index = lax.axis_index("dp")
    even_steps = list(range(2, members, 2))

    own_adapter = jnp.concatenate([adapter_down_maps[0], adapter_up_maps[0]], axis=1)
    by_step = {0: own_adapter}
    for step in even_steps:
        by_step[step] = lax.ppermute(own_adapter, "fsdp", xor_pairs(members, step))
    same_parity = jnp.stack([by_step[step] for step in range(0, members, 2)])
    other_parity = lax.ppermute(same_parity, "fsdp", xor_pairs(members, 1))
    for index, step in enumerate(range(0, members, 2)):
        by_step[step ^ 1] = other_parity[index]
    adapter_stack = jnp.stack([by_step[step] for step in range(members)])

    slot_ids = jnp.take(tenant_owner_slot, block_tenant_ids)
    member_ids = slot_ids // groups
    picked = jnp.stack([lax.dynamic_index_in_dim(adapter_stack, me ^ member_ids[b], 0, keepdims=False)
                        for b in range(blocks)])
    down_block = picked[:, :, :model_width]
    up_block = picked[:, :, model_width:]

    live_rows = (jnp.arange(block_length)[None, :] < block_live_rows[:, None]).astype(jnp.float32)
    live_column = live_rows[:, :, None]
    token_blocks = tokens.reshape(blocks, block_length, model_width)
    cot_blocks = output_gradient.reshape(blocks, block_length, value_width)

    low_rank_state = (
        jnp.einsum("cvj,coj->cvo", token_blocks, down_block, preferred_element_type=jnp.float32)
        * live_column
    ).astype(jnp.bfloat16)
    low_rank_gradient = (
        ADAPTER_SCALE
        * jnp.einsum("btv,bkv->btk", cot_blocks, up_block, preferred_element_type=jnp.float32)
        * live_column
    ).astype(jnp.bfloat16)

    partial_down = jnp.einsum(
        "vio,vih->voh", low_rank_gradient, token_blocks, preferred_element_type=jnp.float32
    )
    partial_up = ADAPTER_SCALE * jnp.einsum(
        "btk,btv->bkv", low_rank_state, cot_blocks, preferred_element_type=jnp.float32
    )
    partial = jnp.concatenate([partial_down, partial_up], axis=2)

    def table_row(member):
        row = jnp.zeros(partial.shape[1:], jnp.float32)
        for b in range(blocks):
            row = row + jnp.where(member_ids[b] == member, partial[b], 0.0)
        return row.astype(jnp.bfloat16)

    sibling = me ^ 1
    for_sibling = jnp.stack([table_row(sibling ^ step) for step in range(0, members, 2)])
    from_sibling = lax.ppermute(for_sibling, "fsdp", xor_pairs(members, 1))
    pair_sums = [
        table_row(me ^ step).astype(jnp.float32) + from_sibling[index].astype(jnp.float32)
        for index, step in enumerate(range(0, members, 2))
    ]
    weight_pieces = relay_gather(frozen_value_weight, members, groups, me, dp_index)
    if weight_pieces and len(weight_pieces[0]) == 2:
        weight_pieces = [(source, 0, value) for source, value in weight_pieces]
    last_pieces = (weight_pieces[6][2],)
    grad_sum = pair_sums[0]
    for index, step in enumerate(even_steps):
        sent = pair_sums[index + 1].astype(jnp.bfloat16)
        sent, _ = lax.optimization_barrier((sent, last_pieces))
        grad_sum = grad_sum + lax.ppermute(sent, "fsdp", xor_pairs(members, step)).astype(jnp.float32)
    grad_sum = grad_sum.astype(jnp.bfloat16)
    grad_down = grad_sum[None, :, :model_width]
    grad_up = grad_sum[None, :, model_width:]

    adapter_output = jnp.einsum(
        "znr,zrm->znm", low_rank_state, up_block, preferred_element_type=jnp.float32
    ).reshape(tok_rows, value_width)
    live_flat = live_rows.reshape(tok_rows, 1)
    masked_cot = (output_gradient * live_flat).astype(jnp.bfloat16)

    output_total = ADAPTER_SCALE * adapter_output
    token_gradient = jnp.zeros((tok_rows, model_width), jnp.bfloat16)
    for source, chunk, weight_piece in weight_pieces:
        piece_rows = weight_piece.shape[0]
        column = source * shard_rows + chunk * piece_rows
        token_piece = lax.dynamic_slice_in_dim(tokens, column, piece_rows, axis=1)
        output_total = lax.optimization_barrier(output_total + jnp.dot(
            token_piece, weight_piece, preferred_element_type=jnp.float32
        ))
        down_piece = lax.dynamic_slice_in_dim(down_block, column, piece_rows, axis=2)
        backward_piece = lax.dot_general(
            masked_cot, weight_piece, (((1,), (1,)), ((), ())), preferred_element_type=jnp.float32
        ) + jnp.einsum(
            "uio,uof->uif", low_rank_gradient, down_piece, preferred_element_type=jnp.float32
        ).reshape(tok_rows, piece_rows)
        token_gradient = lax.dynamic_update_slice_in_dim(
            token_gradient, backward_piece.astype(jnp.bfloat16), column, axis=1
        )
    output = (live_flat * output_total).astype(jnp.bfloat16)
    return (output, token_gradient, grad_down, grad_up)


def solution(mesh):
    placed = (
        P(("fsdp", "dp"), None),
        P(("fsdp", "dp"), None),
        P("fsdp", None),
        P(("fsdp", "dp"), None, None),
        P(("fsdp", "dp"), None, None),
        P(("fsdp", "dp")),
        P(("fsdp", "dp")),
        P(),
    )
    return jax.shard_map(
        on_device,
        mesh=mesh,
        in_specs=placed,
        out_specs=(
            P(("fsdp", "dp"), None),
            P(("fsdp", "dp"), None),
            P(("fsdp", "dp"), None, None),
            P(("fsdp", "dp"), None, None),
        ),
        check_vma=False,
    )
```

```python
import jax
import jax.numpy as jnp
from jax import lax
from jax.sharding import PartitionSpec as P

ADAPTER_SCALE = 2.0
WEIGHT_CHUNKS = 2


def xor_pairs(count, step):
    return [(src, src ^ step) for src in range(count)]


def relay_gather(shard, members, groups, me, dp_index):
    flat = members * groups
    parity = me % 2
    if members != 8 or groups % 2 != 0:
        parts = {0: shard}
        for step in range(2, members, 2):
            parts[step] = lax.ppermute(shard, "fsdp", xor_pairs(members, step))
        for step in range(0, members, 2):
            parts[step + 1] = lax.ppermute(parts[step], "fsdp", xor_pairs(members, 1))
        return [(me ^ step, parts[step]) for step in range(members)]

    def flat_pairs(target):
        pairs = []
        for i in range(members):
            for d in range(groups):
                role = (i % 2) ^ (d % 2)
                ti, td = target(i, d, role)
                pairs.append((i * groups + d, ti * groups + td))
        return pairs

    first_pairs = flat_pairs(lambda i, d, role: (i ^ (2 + 2 * role), d))
    relay_pairs = flat_pairs(lambda i, d, role: (i ^ (4 - 2 * role), d))
    partner_pairs = flat_pairs(lambda i, d, role: (i, d ^ 1))
    role = parity ^ (dp_index % 2)
    sibling = me ^ 1
    sibling_role = 1 - role
    sources = [me, me ^ (2 + 2 * role), me ^ 6, me ^ (4 - 2 * role)]
    sibling_sources = [sibling, sibling ^ (2 + 2 * sibling_role), sibling ^ 6,
                       sibling ^ (4 - 2 * sibling_role)]
    rows = shard.shape[0] // WEIGHT_CHUNKS
    result = []
    previous = None
    for k in range(WEIGHT_CHUNKS):
        piece = shard[k * rows:(k + 1) * rows]
        result.append((0.0, sources[0], k, piece))
        result.append((1.0, sibling_sources[0], k, lax.ppermute(piece, "fsdp", xor_pairs(members, 1))))
        if previous is not None:
            piece, _ = lax.optimization_barrier((piece, previous))
        first = lax.ppermute(piece, ("fsdp", "dp"), first_pairs)
        previous = first
        result.append((2.0 + 2 * k, sources[1], k, first))
        result.append((3.0 + 2 * k, sibling_sources[1], k, lax.ppermute(first, "fsdp", xor_pairs(members, 1))))
        relayed = lax.ppermute(first, ("fsdp", "dp"), relay_pairs)
        partner = lax.ppermute(first, ("fsdp", "dp"), partner_pairs)
        result.append((4.5 + 2 * k, sources[2], k, relayed))
        result.append((4.5 + 2 * k, sources[3], k, partner))
        late = lax.ppermute(jnp.stack([relayed, partner]), "fsdp", xor_pairs(members, 1))
        result.append((5.5 + 2 * k, sibling_sources[2], k, late[0]))
        result.append((5.5 + 2 * k, sibling_sources[3], k, late[1]))
    result.sort(key=lambda item: item[0])
    return [item[1:] for item in result]


def on_device(
    tokens,
    output_gradient,
    frozen_value_weight,
    adapter_down_maps,
    adapter_up_maps,
    block_tenant_ids,
    block_live_rows,
    tenant_owner_slot,
):
    tok_rows, model_width = tokens.shape
    value_width = output_gradient.shape[1]
    blocks = block_tenant_ids.shape[0]
    block_length = tok_rows // blocks
    groups = lax.axis_size("dp")
    members = lax.axis_size("fsdp")
    shard_rows = frozen_value_weight.shape[0]
    me = lax.axis_index("fsdp")
    dp_index = lax.axis_index("dp")
    even_steps = list(range(2, members, 2))

    own_adapter = jnp.concatenate([adapter_down_maps[0], adapter_up_maps[0]], axis=1)
    by_step = {0: own_adapter}
    for step in even_steps:
        by_step[step] = lax.ppermute(own_adapter, "fsdp", xor_pairs(members, step))
    same_parity = jnp.stack([by_step[step] for step in range(0, members, 2)])
    other_parity = lax.ppermute(same_parity, "fsdp", xor_pairs(members, 1))
    for index, step in enumerate(range(0, members, 2)):
        by_step[step ^ 1] = other_parity[index]
    adapter_stack = jnp.stack([by_step[step] for step in range(members)])

    slot_ids = jnp.take(tenant_owner_slot, block_tenant_ids)
    member_ids = slot_ids // groups
    picked = jnp.stack([lax.dynamic_index_in_dim(adapter_stack, me ^ member_ids[b], 0, keepdims=False)
                        for b in range(blocks)])
    down_block = picked[:, :, :model_width]
    up_block = picked[:, :, model_width:]

    live_rows = (jnp.arange(block_length)[None, :] < block_live_rows[:, None]).astype(jnp.float32)
    live_column = live_rows[:, :, None]
    token_blocks = tokens.reshape(blocks, block_length, model_width)
    cot_blocks = output_gradient.reshape(blocks, block_length, value_width)

    low_rank_state = (
        jnp.einsum("cvj,coj->cvo", token_blocks, down_block, preferred_element_type=jnp.float32)
        * live_column
    ).astype(jnp.bfloat16)
    low_rank_gradient = (
        ADAPTER_SCALE
        * jnp.einsum("btv,bkv->btk", cot_blocks, up_block, preferred_element_type=jnp.float32)
        * live_column
    ).astype(jnp.bfloat16)

    partial_down = jnp.einsum(
        "vio,vih->voh", low_rank_gradient, token_blocks, preferred_element_type=jnp.float32
    )
    partial_up = ADAPTER_SCALE * jnp.einsum(
        "btk,btv->bkv", low_rank_state, cot_blocks, preferred_element_type=jnp.float32
    )
    partial = jnp.concatenate([partial_down, partial_up], axis=2)

    def table_row(member):
        row = jnp.zeros(partial.shape[1:], jnp.float32)
        for b in range(blocks):
            row = row + jnp.where(member_ids[b] == member, partial[b], 0.0)
        return row.astype(jnp.bfloat16)

    sibling = me ^ 1
    for_sibling = jnp.stack([table_row(sibling ^ step) for step in range(0, members, 2)])
    from_sibling = lax.ppermute(for_sibling, "fsdp", xor_pairs(members, 1))
    pair_sums = [
        table_row(me ^ step).astype(jnp.float32) + from_sibling[index].astype(jnp.float32)
        for index, step in enumerate(range(0, members, 2))
    ]
    weight_pieces = relay_gather(frozen_value_weight, members, groups, me, dp_index)
    if weight_pieces and len(weight_pieces[0]) == 2:
        weight_pieces = [(source, 0, value) for source, value in weight_pieces]
    last_pieces = (weight_pieces[-4][2],)
    grad_sum = pair_sums[0]
    for index, step in enumerate(even_steps):
        sent = pair_sums[index + 1].astype(jnp.bfloat16)
        sent, _ = lax.optimization_barrier((sent, last_pieces))
        grad_sum = grad_sum + lax.ppermute(sent, "fsdp", xor_pairs(members, step)).astype(jnp.float32)
    grad_sum = grad_sum.astype(jnp.bfloat16)
    grad_down = grad_sum[None, :, :model_width]
    grad_up = grad_sum[None, :, model_width:]

    adapter_output = jnp.einsum(
        "znr,zrm->znm", low_rank_state, up_block, preferred_element_type=jnp.float32
    ).reshape(tok_rows, value_width)
    live_flat = live_rows.reshape(tok_rows, 1)
    masked_cot = (output_gradient * live_flat).astype(jnp.bfloat16)

    output_total = ADAPTER_SCALE * adapter_output
    token_gradient = jnp.zeros((tok_rows, model_width), jnp.bfloat16)
    for source, chunk, weight_piece in weight_pieces:
        piece_rows = weight_piece.shape[0]
        column = source * shard_rows + chunk * piece_rows
        token_piece = lax.dynamic_slice_in_dim(tokens, column, piece_rows, axis=1)
        output_total = lax.optimization_barrier(output_total + jnp.dot(
            token_piece, weight_piece, preferred_element_type=jnp.float32
        ))
        down_piece = lax.dynamic_slice_in_dim(down_block, column, piece_rows, axis=2)
        backward_piece = lax.dot_general(
            masked_cot, weight_piece, (((1,), (1,)), ((), ())), preferred_element_type=jnp.float32
        ) + jnp.einsum(
            "uio,uof->uif", low_rank_gradient, down_piece, preferred_element_type=jnp.float32
        ).reshape(tok_rows, piece_rows)
        token_gradient = lax.dynamic_update_slice_in_dim(
            token_gradient, backward_piece.astype(jnp.bfloat16), column, axis=1
        )
    output = (live_flat * output_total).astype(jnp.bfloat16)
    return (output, token_gradient, grad_down, grad_up)


def solution(mesh):
    placed = (
        P(("fsdp", "dp"), None),
        P(("fsdp", "dp"), None),
        P("fsdp", None),
        P(("fsdp", "dp"), None, None),
        P(("fsdp", "dp"), None, None),
        P(("fsdp", "dp")),
        P(("fsdp", "dp")),
        P(),
    )
    return jax.shard_map(
        on_device,
        mesh=mesh,
        in_specs=placed,
        out_specs=(
            P(("fsdp", "dp"), None),
            P(("fsdp", "dp"), None),
            P(("fsdp", "dp"), None, None),
            P(("fsdp", "dp"), None, None),
        ),
        check_vma=False,
    )
```

```python
import jax
import jax.numpy as jnp
from jax import lax
from jax.sharding import PartitionSpec as P

ADAPTER_SCALE = 2.0
WEIGHT_CHUNKS = 2


def xor_pairs(count, step):
    return [(src, src ^ step) for src in range(count)]


def relay_gather(shard, members, groups, me, dp_index):
    flat = members * groups
    parity = me % 2
    if members != 8 or groups % 2 != 0:
        parts = {0: shard}
        for step in range(2, members, 2):
            parts[step] = lax.ppermute(shard, "fsdp", xor_pairs(members, step))
        for step in range(0, members, 2):
            parts[step + 1] = lax.ppermute(parts[step], "fsdp", xor_pairs(members, 1))
        return [(me ^ step, parts[step]) for step in range(members)]

    def flat_pairs(target):
        pairs = []
        for i in range(members):
            for d in range(groups):
                role = (i % 2) ^ (d % 2)
                ti, td = target(i, d, role)
                pairs.append((i * groups + d, ti * groups + td))
        return pairs

    first_pairs = flat_pairs(lambda i, d, role: (i ^ (2 + 2 * role), d))
    relay_pairs = flat_pairs(lambda i, d, role: (i ^ (4 - 2 * role), d))
    partner_pairs = flat_pairs(lambda i, d, role: (i, d ^ 1))
    role = parity ^ (dp_index % 2)
    sibling = me ^ 1
    sibling_role = 1 - role
    sources = [me, me ^ (2 + 2 * role), me ^ 6, me ^ (4 - 2 * role)]
    sibling_sources = [sibling, sibling ^ (2 + 2 * sibling_role), sibling ^ 6,
                       sibling ^ (4 - 2 * sibling_role)]
    rows = shard.shape[0] // WEIGHT_CHUNKS
    result = []
    previous = None
    for k in range(WEIGHT_CHUNKS):
        piece = shard[k * rows:(k + 1) * rows]
        result.append((0.0, sources[0], k, piece))
        result.append((1.0, sibling_sources[0], k, lax.ppermute(piece, "fsdp", xor_pairs(members, 1))))
        if previous is not None:
            piece, _ = lax.optimization_barrier((piece, previous))
        first = lax.ppermute(piece, ("fsdp", "dp"), first_pairs)
        previous = first
        result.append((2.0 + 2 * k, sources[1], k, first))
        result.append((3.0 + 2 * k, sibling_sources[1], k, lax.ppermute(first, "fsdp", xor_pairs(members, 1))))
        relayed = lax.ppermute(first, ("fsdp", "dp"), relay_pairs)
        partner = lax.ppermute(first, ("fsdp", "dp"), partner_pairs)
        result.append((4.5 + 2 * k, sources[2], k, relayed))
        result.append((4.5 + 2 * k, sources[3], k, partner))
        result.append((5.5 + 2 * k, sibling_sources[2], k,
                       lax.ppermute(relayed, "fsdp", xor_pairs(members, 1))))
        result.append((5.5 + 2 * k, sibling_sources[3], k,
                       lax.ppermute(partner, "fsdp", xor_pairs(members, 1))))
    result.sort(key=lambda item: item[0])
    return [item[1:] for item in result]


def on_device(
    tokens,
    output_gradient,
    frozen_value_weight,
    adapter_down_maps,
    adapter_up_maps,
    block_tenant_ids,
    block_live_rows,
    tenant_owner_slot,
):
    tok_rows, model_width = tokens.shape
    value_width = output_gradient.shape[1]
    blocks = block_tenant_ids.shape[0]
    block_length = tok_rows // blocks
    groups = lax.axis_size("dp")
    members = lax.axis_size("fsdp")
    shard_rows = frozen_value_weight.shape[0]
    me = lax.axis_index("fsdp")
    dp_index = lax.axis_index("dp")
    even_steps = list(range(2, members, 2))

    own_adapter = jnp.concatenate([adapter_down_maps[0], adapter_up_maps[0]], axis=1)
    by_step = {0: own_adapter}
    for step in even_steps:
        by_step[step] = lax.ppermute(own_adapter, "fsdp", xor_pairs(members, step))
    same_parity = jnp.stack([by_step[step] for step in range(0, members, 2)])
    other_parity = lax.ppermute(same_parity, "fsdp", xor_pairs(members, 1))
    for index, step in enumerate(range(0, members, 2)):
        by_step[step ^ 1] = other_parity[index]
    adapter_stack = jnp.stack([by_step[step] for step in range(members)])

    slot_ids = jnp.take(tenant_owner_slot, block_tenant_ids)
    member_ids = slot_ids // groups
    picked = jnp.stack([lax.dynamic_index_in_dim(adapter_stack, me ^ member_ids[b], 0, keepdims=False)
                        for b in range(blocks)])
    down_block = picked[:, :, :model_width]
    up_block = picked[:, :, model_width:]

    live_rows = (jnp.arange(block_length)[None, :] < block_live_rows[:, None]).astype(jnp.float32)
    live_column = live_rows[:, :, None]
    token_blocks = tokens.reshape(blocks, block_length, model_width)
    cot_blocks = output_gradient.reshape(blocks, block_length, value_width)

    low_rank_state = (
        jnp.einsum("cvj,coj->cvo", token_blocks, down_block, preferred_element_type=jnp.float32)
        * live_column
    ).astype(jnp.bfloat16)
    low_rank_gradient = (
        ADAPTER_SCALE
        * jnp.einsum("btv,bkv->btk", cot_blocks, up_block, preferred_element_type=jnp.float32)
        * live_column
    ).astype(jnp.bfloat16)

    partial_down = jnp.einsum(
        "vio,vih->voh", low_rank_gradient, token_blocks, preferred_element_type=jnp.float32
    )
    partial_up = ADAPTER_SCALE * jnp.einsum(
        "btk,btv->bkv", low_rank_state, cot_blocks, preferred_element_type=jnp.float32
    )
    partial = jnp.concatenate([partial_down, partial_up], axis=2)

    def table_row(member):
        row = jnp.zeros(partial.shape[1:], jnp.float32)
        for b in range(blocks):
            row = row + jnp.where(member_ids[b] == member, partial[b], 0.0)
        return row.astype(jnp.bfloat16)

    sibling = me ^ 1
    for_sibling = jnp.stack([table_row(sibling ^ step) for step in range(0, members, 2)])
    from_sibling = lax.ppermute(for_sibling, "fsdp", xor_pairs(members, 1))
    pair_sums = [
        table_row(me ^ step).astype(jnp.float32) + from_sibling[index].astype(jnp.float32)
        for index, step in enumerate(range(0, members, 2))
    ]
    weight_pieces = relay_gather(frozen_value_weight, members, groups, me, dp_index)
    if weight_pieces and len(weight_pieces[0]) == 2:
        weight_pieces = [(source, 0, value) for source, value in weight_pieces]
    last_pieces = (weight_pieces[-4][2],)
    grad_sum = pair_sums[0]
    for index, step in enumerate(even_steps):
        sent = pair_sums[index + 1].astype(jnp.bfloat16)
        sent, _ = lax.optimization_barrier((sent, last_pieces))
        grad_sum = grad_sum + lax.ppermute(sent, "fsdp", xor_pairs(members, step)).astype(jnp.float32)
    grad_sum = grad_sum.astype(jnp.bfloat16)
    grad_down = grad_sum[None, :, :model_width]
    grad_up = grad_sum[None, :, model_width:]

    adapter_output = jnp.einsum(
        "znr,zrm->znm", low_rank_state, up_block, preferred_element_type=jnp.float32
    ).reshape(tok_rows, value_width)
    live_flat = live_rows.reshape(tok_rows, 1)
    masked_cot = (output_gradient * live_flat).astype(jnp.bfloat16)

    output_total = ADAPTER_SCALE * adapter_output
    token_gradient = jnp.zeros((tok_rows, model_width), jnp.bfloat16)
    for source, chunk, weight_piece in weight_pieces:
        piece_rows = weight_piece.shape[0]
        column = source * shard_rows + chunk * piece_rows
        token_piece = lax.dynamic_slice_in_dim(tokens, column, piece_rows, axis=1)
        output_total = lax.optimization_barrier(output_total + jnp.dot(
            token_piece, weight_piece, preferred_element_type=jnp.float32
        ))
        down_piece = lax.dynamic_slice_in_dim(down_block, column, piece_rows, axis=2)
        backward_piece = lax.dot_general(
            masked_cot, weight_piece, (((1,), (1,)), ((), ())), preferred_element_type=jnp.float32
        ) + jnp.einsum(
            "uio,uof->uif", low_rank_gradient, down_piece, preferred_element_type=jnp.float32
        ).reshape(tok_rows, piece_rows)
        token_gradient = lax.dynamic_update_slice_in_dim(
            token_gradient, backward_piece.astype(jnp.bfloat16), column, axis=1
        )
    output = (live_flat * output_total).astype(jnp.bfloat16)
    return (output, token_gradient, grad_down, grad_up)


def solution(mesh):
    placed = (
        P(("fsdp", "dp"), None),
        P(("fsdp", "dp"), None),
        P("fsdp", None),
        P(("fsdp", "dp"), None, None),
        P(("fsdp", "dp"), None, None),
        P(("fsdp", "dp")),
        P(("fsdp", "dp")),
        P(),
    )
    return jax.shard_map(
        on_device,
        mesh=mesh,
        in_specs=placed,
        out_specs=(
            P(("fsdp", "dp"), None),
            P(("fsdp", "dp"), None),
            P(("fsdp", "dp"), None, None),
            P(("fsdp", "dp"), None, None),
        ),
        check_vma=False,
    )
```

```python
import jax
import jax.numpy as jnp
from jax import lax
from jax.sharding import PartitionSpec as P

ADAPTER_SCALE = 2.0


def xor_pairs(count, step):
    return [(src, src ^ step) for src in range(count)]


def relay_gather(shard, members, groups, me, dp_index):
    flat = members * groups
    parity = me % 2
    if members != 8 or groups % 2 != 0:
        parts = {0: shard}
        for step in range(2, members, 2):
            parts[step] = lax.ppermute(shard, "fsdp", xor_pairs(members, step))
        for step in range(0, members, 2):
            parts[step + 1] = lax.ppermute(parts[step], "fsdp", xor_pairs(members, 1))
        return [(me ^ step, parts[step]) for step in range(members)]

    def flat_pairs(target):
        pairs = []
        for i in range(members):
            for d in range(groups):
                role = (i % 2) ^ (d % 2)
                ti, td = target(i, d, role)
                pairs.append((i * groups + d, ti * groups + td))
        return pairs

    first_pairs = flat_pairs(lambda i, d, role: (i ^ (2 + 2 * role), d))
    relay_pairs = flat_pairs(lambda i, d, role: (i ^ (4 - 2 * role), d))
    partner_pairs = flat_pairs(lambda i, d, role: (i, d ^ 1))
    role = parity ^ (dp_index % 2)
    sibling = me ^ 1
    sibling_role = 1 - role
    sources = [me, me ^ (2 + 2 * role), me ^ 6, me ^ (4 - 2 * role)]
    sibling_sources = [sibling, sibling ^ (2 + 2 * sibling_role), sibling ^ 6,
                       sibling ^ (4 - 2 * sibling_role)]
    bounds = [0, 3 * shard.shape[0] // 4, shard.shape[0]]
    result = []
    previous = None
    for k in range(len(bounds) - 1):
        piece = shard[bounds[k]:bounds[k + 1]]
        result.append((0.0, sources[0], bounds[k], piece))
        result.append((1.0, sibling_sources[0], bounds[k], lax.ppermute(piece, "fsdp", xor_pairs(members, 1))))
        if previous is not None:
            piece, _ = lax.optimization_barrier((piece, previous))
        first = lax.ppermute(piece, ("fsdp", "dp"), first_pairs)
        previous = first
        result.append((2.0 + 2 * k, sources[1], bounds[k], first))
        result.append((3.0 + 2 * k, sibling_sources[1], bounds[k], lax.ppermute(first, "fsdp", xor_pairs(members, 1))))
        relayed = lax.ppermute(first, ("fsdp", "dp"), relay_pairs)
        partner = lax.ppermute(first, ("fsdp", "dp"), partner_pairs)
        result.append((4.5 + 2 * k, sources[2], bounds[k], relayed))
        result.append((4.5 + 2 * k, sources[3], bounds[k], partner))
        result.append((5.5 + 2 * k, sibling_sources[2], bounds[k],
                       lax.ppermute(relayed, "fsdp", xor_pairs(members, 1))))
        result.append((5.5 + 2 * k, sibling_sources[3], bounds[k],
                       lax.ppermute(partner, "fsdp", xor_pairs(members, 1))))
    result.sort(key=lambda item: item[0])
    return [item[1:] for item in result]


def on_device(
    tokens,
    output_gradient,
    frozen_value_weight,
    adapter_down_maps,
    adapter_up_maps,
    block_tenant_ids,
    block_live_rows,
    tenant_owner_slot,
):
    tok_rows, model_width = tokens.shape
    value_width = output_gradient.shape[1]
    blocks = block_tenant_ids.shape[0]
    block_length = tok_rows // blocks
    groups = lax.axis_size("dp")
    members = lax.axis_size("fsdp")
    shard_rows = frozen_value_weight.shape[0]
    me = lax.axis_index("fsdp")
    dp_index = lax.axis_index("dp")
    even_steps = list(range(2, members, 2))

    own_adapter = jnp.concatenate([adapter_down_maps[0], adapter_up_maps[0]], axis=1)
    by_step = {0: own_adapter}
    for step in even_steps:
        by_step[step] = lax.ppermute(own_adapter, "fsdp", xor_pairs(members, step))
    same_parity = jnp.stack([by_step[step] for step in range(0, members, 2)])
    other_parity = lax.ppermute(same_parity, "fsdp", xor_pairs(members, 1))
    for index, step in enumerate(range(0, members, 2)):
        by_step[step ^ 1] = other_parity[index]
    adapter_stack = jnp.stack([by_step[step] for step in range(members)])

    slot_ids = jnp.take(tenant_owner_slot, block_tenant_ids)
    member_ids = slot_ids // groups
    picked = jnp.stack([lax.dynamic_index_in_dim(adapter_stack, me ^ member_ids[b], 0, keepdims=False)
                        for b in range(blocks)])
    down_block = picked[:, :, :model_width]
    up_block = picked[:, :, model_width:]

    live_rows = (jnp.arange(block_length)[None, :] < block_live_rows[:, None]).astype(jnp.float32)
    live_column = live_rows[:, :, None]
    token_blocks = tokens.reshape(blocks, block_length, model_width)
    cot_blocks = output_gradient.reshape(blocks, block_length, value_width)

    low_rank_state = (
        jnp.einsum("cvj,coj->cvo", token_blocks, down_block, preferred_element_type=jnp.float32)
        * live_column
    ).astype(jnp.bfloat16)
    low_rank_gradient = (
        ADAPTER_SCALE
        * jnp.einsum("btv,bkv->btk", cot_blocks, up_block, preferred_element_type=jnp.float32)
        * live_column
    ).astype(jnp.bfloat16)

    partial_down = jnp.einsum(
        "vio,vih->voh", low_rank_gradient, token_blocks, preferred_element_type=jnp.float32
    )
    partial_up = ADAPTER_SCALE * jnp.einsum(
        "btk,btv->bkv", low_rank_state, cot_blocks, preferred_element_type=jnp.float32
    )
    partial = jnp.concatenate([partial_down, partial_up], axis=2)

    def table_row(member):
        row = jnp.zeros(partial.shape[1:], jnp.float32)
        for b in range(blocks):
            row = row + jnp.where(member_ids[b] == member, partial[b], 0.0)
        return row.astype(jnp.bfloat16)

    sibling = me ^ 1
    for_sibling = jnp.stack([table_row(sibling ^ step) for step in range(0, members, 2)])
    from_sibling = lax.ppermute(for_sibling, "fsdp", xor_pairs(members, 1))
    pair_sums = [
        table_row(me ^ step).astype(jnp.float32) + from_sibling[index].astype(jnp.float32)
        for index, step in enumerate(range(0, members, 2))
    ]
    weight_pieces = relay_gather(frozen_value_weight, members, groups, me, dp_index)
    if weight_pieces and len(weight_pieces[0]) == 2:
        weight_pieces = [(source, 0, value) for source, value in weight_pieces]
    last_pieces = (weight_pieces[-4][2],)
    grad_sum = pair_sums[0]
    for index, step in enumerate(even_steps):
        sent = pair_sums[index + 1].astype(jnp.bfloat16)
        sent, _ = lax.optimization_barrier((sent, last_pieces))
        grad_sum = grad_sum + lax.ppermute(sent, "fsdp", xor_pairs(members, step)).astype(jnp.float32)
    grad_sum = grad_sum.astype(jnp.bfloat16)
    grad_down = grad_sum[None, :, :model_width]
    grad_up = grad_sum[None, :, model_width:]

    adapter_output = jnp.einsum(
        "znr,zrm->znm", low_rank_state, up_block, preferred_element_type=jnp.float32
    ).reshape(tok_rows, value_width)
    live_flat = live_rows.reshape(tok_rows, 1)
    masked_cot = (output_gradient * live_flat).astype(jnp.bfloat16)

    output_total = ADAPTER_SCALE * adapter_output
    token_gradient = jnp.zeros((tok_rows, model_width), jnp.bfloat16)
    for source, chunk, weight_piece in weight_pieces:
        piece_rows = weight_piece.shape[0]
        column = source * shard_rows + chunk
        token_piece = lax.dynamic_slice_in_dim(tokens, column, piece_rows, axis=1)
        output_total = lax.optimization_barrier(output_total + jnp.dot(
            token_piece, weight_piece, preferred_element_type=jnp.float32
        ))
        down_piece = lax.dynamic_slice_in_dim(down_block, column, piece_rows, axis=2)
        backward_piece = lax.dot_general(
            masked_cot, weight_piece, (((1,), (1,)), ((), ())), preferred_element_type=jnp.float32
        ) + jnp.einsum(
            "uio,uof->uif", low_rank_gradient, down_piece, preferred_element_type=jnp.float32
        ).reshape(tok_rows, piece_rows)
        token_gradient = lax.dynamic_update_slice_in_dim(
            token_gradient, backward_piece.astype(jnp.bfloat16), column, axis=1
        )
    output = (live_flat * output_total).astype(jnp.bfloat16)
    return (output, token_gradient, grad_down, grad_up)


def solution(mesh):
    placed = (
        P(("fsdp", "dp"), None),
        P(("fsdp", "dp"), None),
        P("fsdp", None),
        P(("fsdp", "dp"), None, None),
        P(("fsdp", "dp"), None, None),
        P(("fsdp", "dp")),
        P(("fsdp", "dp")),
        P(),
    )
    return jax.shard_map(
        on_device,
        mesh=mesh,
        in_specs=placed,
        out_specs=(
            P(("fsdp", "dp"), None),
            P(("fsdp", "dp"), None),
            P(("fsdp", "dp"), None, None),
            P(("fsdp", "dp"), None, None),
        ),
        check_vma=False,
    )
```

```python
import jax
import jax.numpy as jnp
from jax import lax
from jax.sharding import PartitionSpec as P

ADAPTER_SCALE = 2.0
WEIGHT_CHUNKS = 2


def xor_pairs(count, step):
    return [(src, src ^ step) for src in range(count)]


def relay_gather(shard, members, groups, me, dp_index):
    flat = members * groups
    parity = me % 2
    if members != 8 or groups % 2 != 0:
        parts = {0: shard}
        for step in range(2, members, 2):
            parts[step] = lax.ppermute(shard, "fsdp", xor_pairs(members, step))
        for step in range(0, members, 2):
            parts[step + 1] = lax.ppermute(parts[step], "fsdp", xor_pairs(members, 1))
        return [(me ^ step, parts[step]) for step in range(members)]

    def flat_pairs(target):
        pairs = []
        for i in range(members):
            for d in range(groups):
                role = (i % 2) ^ (d % 2)
                ti, td = target(i, d, role)
                pairs.append((i * groups + d, ti * groups + td))
        return pairs

    first_pairs = flat_pairs(lambda i, d, role: (i ^ (2 + 2 * role), d))
    relay_pairs = flat_pairs(lambda i, d, role: (i ^ (4 - 2 * role), d))
    partner_pairs = flat_pairs(lambda i, d, role: (i, d ^ 1))
    role = parity ^ (dp_index % 2)
    sibling = me ^ 1
    sibling_role = 1 - role
    sources = [me, me ^ (2 + 2 * role), me ^ 6, me ^ (4 - 2 * role)]
    sibling_sources = [sibling, sibling ^ (2 + 2 * sibling_role), sibling ^ 6,
                       sibling ^ (4 - 2 * sibling_role)]
    rows = shard.shape[0] // WEIGHT_CHUNKS
    result = []
    previous = None
    for k in range(WEIGHT_CHUNKS):
        piece = shard[k * rows:(k + 1) * rows]
        result.append((0.0, sources[0], k, piece))
        result.append((1.0, sibling_sources[0], k, lax.ppermute(piece, "fsdp", xor_pairs(members, 1))))
        if previous is not None:
            piece, _ = lax.optimization_barrier((piece, previous))
        first = lax.ppermute(piece, ("fsdp", "dp"), first_pairs)
        previous = first
        result.append((2.0 + 2 * k, sources[1], k, first))
        result.append((3.0 + 2 * k, sibling_sources[1], k, lax.ppermute(first, "fsdp", xor_pairs(members, 1))))
        relayed = lax.ppermute(first, ("fsdp", "dp"), relay_pairs)
        partner = lax.ppermute(first, ("fsdp", "dp"), partner_pairs)
        result.append((4.5 + 2 * k, sources[2], k, relayed))
        result.append((4.5 + 2 * k, sources[3], k, partner))
        result.append((5.5 + 2 * k, sibling_sources[2], k,
                       lax.ppermute(relayed, "fsdp", xor_pairs(members, 1))))
        result.append((5.5 + 2 * k, sibling_sources[3], k,
                       lax.ppermute(partner, "fsdp", xor_pairs(members, 1))))
    result.sort(key=lambda item: item[0])
    return [item[1:] for item in result]


def on_device(
    tokens,
    output_gradient,
    frozen_value_weight,
    adapter_down_maps,
    adapter_up_maps,
    block_tenant_ids,
    block_live_rows,
    tenant_owner_slot,
):
    tok_rows, model_width = tokens.shape
    value_width = output_gradient.shape[1]
    blocks = block_tenant_ids.shape[0]
    block_length = tok_rows // blocks
    groups = lax.axis_size("dp")
    members = lax.axis_size("fsdp")
    shard_rows = frozen_value_weight.shape[0]
    me = lax.axis_index("fsdp")
    dp_index = lax.axis_index("dp")
    even_steps = list(range(2, members, 2))

    own_adapter = jnp.concatenate([adapter_down_maps[0], adapter_up_maps[0]], axis=1)
    by_step = {0: own_adapter}
    for step in even_steps:
        by_step[step] = lax.ppermute(own_adapter, "fsdp", xor_pairs(members, step))
    same_parity = jnp.stack([by_step[step] for step in range(0, members, 2)])
    other_parity = lax.ppermute(same_parity, "fsdp", xor_pairs(members, 1))
    for index, step in enumerate(range(0, members, 2)):
        by_step[step ^ 1] = other_parity[index]
    adapter_stack = jnp.stack([by_step[step] for step in range(members)])

    slot_ids = jnp.take(tenant_owner_slot, block_tenant_ids)
    member_ids = slot_ids // groups
    picked = jnp.stack([lax.dynamic_index_in_dim(adapter_stack, me ^ member_ids[b], 0, keepdims=False)
                        for b in range(blocks)])
    down_block = picked[:, :, :model_width]
    up_block = picked[:, :, model_width:]

    live_rows = (jnp.arange(block_length)[None, :] < block_live_rows[:, None]).astype(jnp.float32)
    live_column = live_rows[:, :, None]
    token_blocks = tokens.reshape(blocks, block_length, model_width)
    cot_blocks = output_gradient.reshape(blocks, block_length, value_width)

    low_rank_state = (
        jnp.einsum("cvj,coj->cvo", token_blocks, down_block, preferred_element_type=jnp.float32)
        * live_column
    ).astype(jnp.bfloat16)
    low_rank_gradient = (
        ADAPTER_SCALE
        * jnp.einsum("btv,bkv->btk", cot_blocks, up_block, preferred_element_type=jnp.float32)
        * live_column
    ).astype(jnp.bfloat16)

    partial_down = jnp.einsum(
        "vio,vih->voh", low_rank_gradient, token_blocks, preferred_element_type=jnp.float32
    )
    partial_up = ADAPTER_SCALE * jnp.einsum(
        "btk,btv->bkv", low_rank_state, cot_blocks, preferred_element_type=jnp.float32
    )
    partial = jnp.concatenate([partial_down, partial_up], axis=2)

    def table_row(member):
        row = jnp.zeros(partial.shape[1:], jnp.float32)
        for b in range(blocks):
            row = row + jnp.where(member_ids[b] == member, partial[b], 0.0)
        return row.astype(jnp.bfloat16)

    sibling = me ^ 1
    for_sibling = jnp.stack([table_row(sibling ^ step) for step in range(0, members, 2)])
    from_sibling = lax.ppermute(for_sibling, "fsdp", xor_pairs(members, 1))
    pair_sums = [
        table_row(me ^ step).astype(jnp.float32) + from_sibling[index].astype(jnp.float32)
        for index, step in enumerate(range(0, members, 2))
    ]
    weight_pieces = relay_gather(frozen_value_weight, members, groups, me, dp_index)
    if weight_pieces and len(weight_pieces[0]) == 2:
        weight_pieces = [(source, 0, value) for source, value in weight_pieces]
    last_pieces = (weight_pieces[-2][2],)
    grad_sum = pair_sums[0]
    for index, step in enumerate(even_steps):
        sent = pair_sums[index + 1].astype(jnp.bfloat16)
        sent, _ = lax.optimization_barrier((sent, last_pieces))
        grad_sum = grad_sum + lax.ppermute(sent, "fsdp", xor_pairs(members, step)).astype(jnp.float32)
    grad_sum = grad_sum.astype(jnp.bfloat16)
    grad_down = grad_sum[None, :, :model_width]
    grad_up = grad_sum[None, :, model_width:]

    adapter_output = jnp.einsum(
        "znr,zrm->znm", low_rank_state, up_block, preferred_element_type=jnp.float32
    ).reshape(tok_rows, value_width)
    live_flat = live_rows.reshape(tok_rows, 1)
    masked_cot = (output_gradient * live_flat).astype(jnp.bfloat16)

    output_total = ADAPTER_SCALE * adapter_output
    token_gradient = jnp.zeros((tok_rows, model_width), jnp.bfloat16)
    for source, chunk, weight_piece in weight_pieces:
        piece_rows = weight_piece.shape[0]
        column = source * shard_rows + chunk * piece_rows
        token_piece = lax.dynamic_slice_in_dim(tokens, column, piece_rows, axis=1)
        output_total = lax.optimization_barrier(output_total + jnp.dot(
            token_piece, weight_piece, preferred_element_type=jnp.float32
        ))
        down_piece = lax.dynamic_slice_in_dim(down_block, column, piece_rows, axis=2)
        backward_piece = lax.dot_general(
            masked_cot, weight_piece, (((1,), (1,)), ((), ())), preferred_element_type=jnp.float32
        ) + jnp.einsum(
            "uio,uof->uif", low_rank_gradient, down_piece, preferred_element_type=jnp.float32
        ).reshape(tok_rows, piece_rows)
        token_gradient = lax.dynamic_update_slice_in_dim(
            token_gradient, backward_piece.astype(jnp.bfloat16), column, axis=1
        )
    output = (live_flat * output_total).astype(jnp.bfloat16)
    return (output, token_gradient, grad_down, grad_up)


def solution(mesh):
    placed = (
        P(("fsdp", "dp"), None),
        P(("fsdp", "dp"), None),
        P("fsdp", None),
        P(("fsdp", "dp"), None, None),
        P(("fsdp", "dp"), None, None),
        P(("fsdp", "dp")),
        P(("fsdp", "dp")),
        P(),
    )
    return jax.shard_map(
        on_device,
        mesh=mesh,
        in_specs=placed,
        out_specs=(
            P(("fsdp", "dp"), None),
            P(("fsdp", "dp"), None),
            P(("fsdp", "dp"), None, None),
            P(("fsdp", "dp"), None, None),
        ),
        check_vma=False,
    )
```

```python
import jax
import jax.numpy as jnp
from jax import lax
from jax.sharding import PartitionSpec as P

ADAPTER_SCALE = 2.0
WEIGHT_CHUNKS = 2


def xor_pairs(count, step):
    return [(src, src ^ step) for src in range(count)]


def relay_gather(shard, members, groups, me, dp_index):
    flat = members * groups
    parity = me % 2
    if members != 8 or groups % 2 != 0:
        parts = {0: shard}
        for step in range(2, members, 2):
            parts[step] = lax.ppermute(shard, "fsdp", xor_pairs(members, step))
        for step in range(0, members, 2):
            parts[step + 1] = lax.ppermute(parts[step], "fsdp", xor_pairs(members, 1))
        return [(me ^ step, parts[step]) for step in range(members)]

    def flat_pairs(target):
        pairs = []
        for i in range(members):
            for d in range(groups):
                role = (i % 2) ^ (d % 2)
                ti, td = target(i, d, role)
                pairs.append((i * groups + d, ti * groups + td))
        return pairs

    first_pairs = flat_pairs(lambda i, d, role: (i ^ (2 + 2 * role), d))
    relay_pairs = flat_pairs(lambda i, d, role: (i ^ (4 - 2 * role), d))
    partner_pairs = flat_pairs(lambda i, d, role: (i, d ^ 1))
    role = parity ^ (dp_index % 2)
    sibling = me ^ 1
    sibling_role = 1 - role
    sources = [me, me ^ (2 + 2 * role), me ^ 6, me ^ (4 - 2 * role)]
    sibling_sources = [sibling, sibling ^ (2 + 2 * sibling_role), sibling ^ 6,
                       sibling ^ (4 - 2 * sibling_role)]
    rows = shard.shape[0] // WEIGHT_CHUNKS
    result = []
    previous = None
    sibling_shard = lax.ppermute(shard, "fsdp", xor_pairs(members, 1))
    for k in range(WEIGHT_CHUNKS):
        piece = shard[k * rows:(k + 1) * rows]
        result.append((0.0, sources[0], k, piece))
        result.append((1.0, sibling_sources[0], k, sibling_shard[k * rows:(k + 1) * rows]))
        if previous is not None:
            piece, _ = lax.optimization_barrier((piece, previous))
        first = lax.ppermute(piece, ("fsdp", "dp"), first_pairs)
        previous = first
        result.append((2.0 + 2 * k, sources[1], k, first))
        result.append((3.0 + 2 * k, sibling_sources[1], k, lax.ppermute(first, "fsdp", xor_pairs(members, 1))))
        relayed = lax.ppermute(first, ("fsdp", "dp"), relay_pairs)
        partner = lax.ppermute(first, ("fsdp", "dp"), partner_pairs)
        result.append((4.5 + 2 * k, sources[2], k, relayed))
        result.append((4.5 + 2 * k, sources[3], k, partner))
        result.append((5.5 + 2 * k, sibling_sources[2], k,
                       lax.ppermute(relayed, "fsdp", xor_pairs(members, 1))))
        result.append((5.5 + 2 * k, sibling_sources[3], k,
                       lax.ppermute(partner, "fsdp", xor_pairs(members, 1))))
    result.sort(key=lambda item: item[0])
    return [item[1:] for item in result]


def on_device(
    tokens,
    output_gradient,
    frozen_value_weight,
    adapter_down_maps,
    adapter_up_maps,
    block_tenant_ids,
    block_live_rows,
    tenant_owner_slot,
):
    tok_rows, model_width = tokens.shape
    value_width = output_gradient.shape[1]
    blocks = block_tenant_ids.shape[0]
    block_length = tok_rows // blocks
    groups = lax.axis_size("dp")
    members = lax.axis_size("fsdp")
    shard_rows = frozen_value_weight.shape[0]
    me = lax.axis_index("fsdp")
    dp_index = lax.axis_index("dp")
    even_steps = list(range(2, members, 2))

    own_adapter = jnp.concatenate([adapter_down_maps[0], adapter_up_maps[0]], axis=1)
    by_step = {0: own_adapter}
    for step in even_steps:
        by_step[step] = lax.ppermute(own_adapter, "fsdp", xor_pairs(members, step))
    same_parity = jnp.stack([by_step[step] for step in range(0, members, 2)])
    other_parity = lax.ppermute(same_parity, "fsdp", xor_pairs(members, 1))
    for index, step in enumerate(range(0, members, 2)):
        by_step[step ^ 1] = other_parity[index]
    adapter_stack = jnp.stack([by_step[step] for step in range(members)])

    slot_ids = jnp.take(tenant_owner_slot, block_tenant_ids)
    member_ids = slot_ids // groups
    picked = jnp.stack([lax.dynamic_index_in_dim(adapter_stack, me ^ member_ids[b], 0, keepdims=False)
                        for b in range(blocks)])
    down_block = picked[:, :, :model_width]
    up_block = picked[:, :, model_width:]

    live_rows = (jnp.arange(block_length)[None, :] < block_live_rows[:, None]).astype(jnp.float32)
    live_column = live_rows[:, :, None]
    token_blocks = tokens.reshape(blocks, block_length, model_width)
    cot_blocks = output_gradient.reshape(blocks, block_length, value_width)

    low_rank_state = (
        jnp.einsum("cvj,coj->cvo", token_blocks, down_block, preferred_element_type=jnp.float32)
        * live_column
    ).astype(jnp.bfloat16)
    low_rank_gradient = (
        ADAPTER_SCALE
        * jnp.einsum("btv,bkv->btk", cot_blocks, up_block, preferred_element_type=jnp.float32)
        * live_column
    ).astype(jnp.bfloat16)

    partial_down = jnp.einsum(
        "vio,vih->voh", low_rank_gradient, token_blocks, preferred_element_type=jnp.float32
    )
    partial_up = ADAPTER_SCALE * jnp.einsum(
        "btk,btv->bkv", low_rank_state, cot_blocks, preferred_element_type=jnp.float32
    )
    partial = jnp.concatenate([partial_down, partial_up], axis=2)

    def table_row(member):
        row = jnp.zeros(partial.shape[1:], jnp.float32)
        for b in range(blocks):
            row = row + jnp.where(member_ids[b] == member, partial[b], 0.0)
        return row.astype(jnp.bfloat16)

    sibling = me ^ 1
    for_sibling = jnp.stack([table_row(sibling ^ step) for step in range(0, members, 2)])
    from_sibling = lax.ppermute(for_sibling, "fsdp", xor_pairs(members, 1))
    pair_sums = [
        table_row(me ^ step).astype(jnp.float32) + from_sibling[index].astype(jnp.float32)
        for index, step in enumerate(range(0, members, 2))
    ]
    weight_pieces = relay_gather(frozen_value_weight, members, groups, me, dp_index)
    if weight_pieces and len(weight_pieces[0]) == 2:
        weight_pieces = [(source, 0, value) for source, value in weight_pieces]
    last_pieces = (weight_pieces[-4][2],)
    grad_sum = pair_sums[0]
    for index, step in enumerate(even_steps):
        sent = pair_sums[index + 1].astype(jnp.bfloat16)
        sent, _ = lax.optimization_barrier((sent, last_pieces))
        grad_sum = grad_sum + lax.ppermute(sent, "fsdp", xor_pairs(members, step)).astype(jnp.float32)
    grad_sum = grad_sum.astype(jnp.bfloat16)
    grad_down = grad_sum[None, :, :model_width]
    grad_up = grad_sum[None, :, model_width:]

    adapter_output = jnp.einsum(
        "znr,zrm->znm", low_rank_state, up_block, preferred_element_type=jnp.float32
    ).reshape(tok_rows, value_width)
    live_flat = live_rows.reshape(tok_rows, 1)
    masked_cot = (output_gradient * live_flat).astype(jnp.bfloat16)

    output_total = ADAPTER_SCALE * adapter_output
    token_gradient = jnp.zeros((tok_rows, model_width), jnp.bfloat16)
    for source, chunk, weight_piece in weight_pieces:
        piece_rows = weight_piece.shape[0]
        column = source * shard_rows + chunk * piece_rows
        token_piece = lax.dynamic_slice_in_dim(tokens, column, piece_rows, axis=1)
        output_total = lax.optimization_barrier(output_total + jnp.dot(
            token_piece, weight_piece, preferred_element_type=jnp.float32
        ))
        down_piece = lax.dynamic_slice_in_dim(down_block, column, piece_rows, axis=2)
        backward_piece = lax.dot_general(
            masked_cot, weight_piece, (((1,), (1,)), ((), ())), preferred_element_type=jnp.float32
        ) + jnp.einsum(
            "uio,uof->uif", low_rank_gradient, down_piece, preferred_element_type=jnp.float32
        ).reshape(tok_rows, piece_rows)
        token_gradient = lax.dynamic_update_slice_in_dim(
            token_gradient, backward_piece.astype(jnp.bfloat16), column, axis=1
        )
    output = (live_flat * output_total).astype(jnp.bfloat16)
    return (output, token_gradient, grad_down, grad_up)


def solution(mesh):
    placed = (
        P(("fsdp", "dp"), None),
        P(("fsdp", "dp"), None),
        P("fsdp", None),
        P(("fsdp", "dp"), None, None),
        P(("fsdp", "dp"), None, None),
        P(("fsdp", "dp")),
        P(("fsdp", "dp")),
        P(),
    )
    return jax.shard_map(
        on_device,
        mesh=mesh,
        in_specs=placed,
        out_specs=(
            P(("fsdp", "dp"), None),
            P(("fsdp", "dp"), None),
            P(("fsdp", "dp"), None, None),
            P(("fsdp", "dp"), None, None),
        ),
        check_vma=False,
    )
```

```python
import jax
import jax.numpy as jnp
from jax import lax
from jax.sharding import PartitionSpec as P

ADAPTER_SCALE = 2.0
WEIGHT_CHUNKS = 2


def xor_pairs(count, step):
    return [(src, src ^ step) for src in range(count)]


def relay_gather(shard, members, groups, me, dp_index):
    flat = members * groups
    parity = me % 2
    if members != 8 or groups % 2 != 0:
        parts = {0: shard}
        for step in range(2, members, 2):
            parts[step] = lax.ppermute(shard, "fsdp", xor_pairs(members, step))
        for step in range(0, members, 2):
            parts[step + 1] = lax.ppermute(parts[step], "fsdp", xor_pairs(members, 1))
        return [(me ^ step, parts[step]) for step in range(members)]

    def flat_pairs(target):
        pairs = []
        for i in range(members):
            for d in range(groups):
                role = (i % 2) ^ (d % 2)
                ti, td = target(i, d, role)
                pairs.append((i * groups + d, ti * groups + td))
        return pairs

    first_pairs = flat_pairs(lambda i, d, role: (i ^ (2 + 2 * role), d))
    relay_pairs = flat_pairs(lambda i, d, role: (i ^ (4 - 2 * role), d))
    partner_pairs = flat_pairs(lambda i, d, role: (i, d ^ 1))
    role = parity ^ (dp_index % 2)
    sibling = me ^ 1
    sibling_role = 1 - role
    sources = [me, me ^ (2 + 2 * role), me ^ 6, me ^ (4 - 2 * role)]
    sibling_sources = [sibling, sibling ^ (2 + 2 * sibling_role), sibling ^ 6,
                       sibling ^ (4 - 2 * sibling_role)]
    rows = shard.shape[0] // WEIGHT_CHUNKS
    result = []
    previous = None
    sibling_shard = lax.ppermute(shard, "fsdp", xor_pairs(members, 1))
    for k in range(WEIGHT_CHUNKS):
        piece = shard[k * rows:(k + 1) * rows]
        result.append((0.0, sources[0], k, piece))
        result.append((1.0, sibling_sources[0], k, sibling_shard[k * rows:(k + 1) * rows]))
        if previous is not None:
            piece, _ = lax.optimization_barrier((piece, previous))
        first = lax.ppermute(piece, ("fsdp", "dp"), first_pairs)
        previous = first
        result.append((2.0 + 2 * k, sources[1], k, first))
        result.append((3.0 + 2 * k, sibling_sources[1], k, lax.ppermute(first, "fsdp", xor_pairs(members, 1))))
        relayed = lax.ppermute(first, ("fsdp", "dp"), relay_pairs)
        partner = lax.ppermute(first, ("fsdp", "dp"), partner_pairs)
        result.append((4.5 + 2 * k, sources[2], k, relayed))
        result.append((4.5 + 2 * k, sources[3], k, partner))
        if k + 1 < WEIGHT_CHUNKS:
            late = lax.ppermute(jnp.stack([relayed, partner]), "fsdp", xor_pairs(members, 1))
            late_pieces = (late[0], late[1])
        else:
            late_pieces = (lax.ppermute(relayed, "fsdp", xor_pairs(members, 1)),
                           lax.ppermute(partner, "fsdp", xor_pairs(members, 1)))
        result.append((5.5 + 2 * k, sibling_sources[2], k, late_pieces[0]))
        result.append((5.5 + 2 * k, sibling_sources[3], k, late_pieces[1]))
    result.sort(key=lambda item: item[0])
    return [item[1:] for item in result]


def on_device(
    tokens,
    output_gradient,
    frozen_value_weight,
    adapter_down_maps,
    adapter_up_maps,
    block_tenant_ids,
    block_live_rows,
    tenant_owner_slot,
):
    tok_rows, model_width = tokens.shape
    value_width = output_gradient.shape[1]
    blocks = block_tenant_ids.shape[0]
    block_length = tok_rows // blocks
    groups = lax.axis_size("dp")
    members = lax.axis_size("fsdp")
    shard_rows = frozen_value_weight.shape[0]
    me = lax.axis_index("fsdp")
    dp_index = lax.axis_index("dp")
    even_steps = list(range(2, members, 2))

    own_adapter = jnp.concatenate([adapter_down_maps[0], adapter_up_maps[0]], axis=1)
    by_step = {0: own_adapter}
    for step in even_steps:
        by_step[step] = lax.ppermute(own_adapter, "fsdp", xor_pairs(members, step))
    same_parity = jnp.stack([by_step[step] for step in range(0, members, 2)])
    other_parity = lax.ppermute(same_parity, "fsdp", xor_pairs(members, 1))
    for index, step in enumerate(range(0, members, 2)):
        by_step[step ^ 1] = other_parity[index]
    adapter_stack = jnp.stack([by_step[step] for step in range(members)])

    slot_ids = jnp.take(tenant_owner_slot, block_tenant_ids)
    member_ids = slot_ids // groups
    picked = jnp.stack([lax.dynamic_index_in_dim(adapter_stack, me ^ member_ids[b], 0, keepdims=False)
                        for b in range(blocks)])
    down_block = picked[:, :, :model_width]
    up_block = picked[:, :, model_width:]

    live_rows = (jnp.arange(block_length)[None, :] < block_live_rows[:, None]).astype(jnp.float32)
    live_column = live_rows[:, :, None]
    token_blocks = tokens.reshape(blocks, block_length, model_width)
    cot_blocks = output_gradient.reshape(blocks, block_length, value_width)

    low_rank_state = (
        jnp.einsum("cvj,coj->cvo", token_blocks, down_block, preferred_element_type=jnp.float32)
        * live_column
    ).astype(jnp.bfloat16)
    low_rank_gradient = (
        ADAPTER_SCALE
        * jnp.einsum("btv,bkv->btk", cot_blocks, up_block, preferred_element_type=jnp.float32)
        * live_column
    ).astype(jnp.bfloat16)

    partial_down = jnp.einsum(
        "vio,vih->voh", low_rank_gradient, token_blocks, preferred_element_type=jnp.float32
    )
    partial_up = ADAPTER_SCALE * jnp.einsum(
        "btk,btv->bkv", low_rank_state, cot_blocks, preferred_element_type=jnp.float32
    )
    partial = jnp.concatenate([partial_down, partial_up], axis=2)

    def table_row(member):
        row = jnp.zeros(partial.shape[1:], jnp.float32)
        for b in range(blocks):
            row = row + jnp.where(member_ids[b] == member, partial[b], 0.0)
        return row.astype(jnp.bfloat16)

    sibling = me ^ 1
    for_sibling = jnp.stack([table_row(sibling ^ step) for step in range(0, members, 2)])
    from_sibling = lax.ppermute(for_sibling, "fsdp", xor_pairs(members, 1))
    pair_sums = [
        table_row(me ^ step).astype(jnp.float32) + from_sibling[index].astype(jnp.float32)
        for index, step in enumerate(range(0, members, 2))
    ]
    weight_pieces = relay_gather(frozen_value_weight, members, groups, me, dp_index)
    if weight_pieces and len(weight_pieces[0]) == 2:
        weight_pieces = [(source, 0, value) for source, value in weight_pieces]
    last_pieces = (weight_pieces[-4][2],)
    grad_sum = pair_sums[0]
    for index, step in enumerate(even_steps):
        sent = pair_sums[index + 1].astype(jnp.bfloat16)
        sent, _ = lax.optimization_barrier((sent, last_pieces))
        grad_sum = grad_sum + lax.ppermute(sent, "fsdp", xor_pairs(members, step)).astype(jnp.float32)
    grad_sum = grad_sum.astype(jnp.bfloat16)
    grad_down = grad_sum[None, :, :model_width]
    grad_up = grad_sum[None, :, model_width:]

    adapter_output = jnp.einsum(
        "znr,zrm->znm", low_rank_state, up_block, preferred_element_type=jnp.float32
    ).reshape(tok_rows, value_width)
    live_flat = live_rows.reshape(tok_rows, 1)
    masked_cot = (output_gradient * live_flat).astype(jnp.bfloat16)

    output_total = ADAPTER_SCALE * adapter_output
    token_gradient = jnp.zeros((tok_rows, model_width), jnp.bfloat16)
    for source, chunk, weight_piece in weight_pieces:
        piece_rows = weight_piece.shape[0]
        column = source * shard_rows + chunk * piece_rows
        token_piece = lax.dynamic_slice_in_dim(tokens, column, piece_rows, axis=1)
        output_total = lax.optimization_barrier(output_total + jnp.dot(
            token_piece, weight_piece, preferred_element_type=jnp.float32
        ))
        down_piece = lax.dynamic_slice_in_dim(down_block, column, piece_rows, axis=2)
        backward_piece = lax.dot_general(
            masked_cot, weight_piece, (((1,), (1,)), ((), ())), preferred_element_type=jnp.float32
        ) + jnp.einsum(
            "uio,uof->uif", low_rank_gradient, down_piece, preferred_element_type=jnp.float32
        ).reshape(tok_rows, piece_rows)
        token_gradient = lax.dynamic_update_slice_in_dim(
            token_gradient, backward_piece.astype(jnp.bfloat16), column, axis=1
        )
    output = (live_flat * output_total).astype(jnp.bfloat16)
    return (output, token_gradient, grad_down, grad_up)


def solution(mesh):
    placed = (
        P(("fsdp", "dp"), None),
        P(("fsdp", "dp"), None),
        P("fsdp", None),
        P(("fsdp", "dp"), None, None),
        P(("fsdp", "dp"), None, None),
        P(("fsdp", "dp")),
        P(("fsdp", "dp")),
        P(),
    )
    return jax.shard_map(
        on_device,
        mesh=mesh,
        in_specs=placed,
        out_specs=(
            P(("fsdp", "dp"), None),
            P(("fsdp", "dp"), None),
            P(("fsdp", "dp"), None, None),
            P(("fsdp", "dp"), None, None),
        ),
        check_vma=False,
    )
```

```python
import jax
import jax.numpy as jnp
from jax import lax
from jax.sharding import PartitionSpec as P

ADAPTER_SCALE = 2.0
WEIGHT_CHUNKS = 2


def xor_pairs(count, step):
    return [(src, src ^ step) for src in range(count)]


def relay_gather(shard, members, groups, me, dp_index):
    flat = members * groups
    parity = me % 2
    if members != 8 or groups % 2 != 0:
        parts = {0: shard}
        for step in range(2, members, 2):
            parts[step] = lax.ppermute(shard, "fsdp", xor_pairs(members, step))
        for step in range(0, members, 2):
            parts[step + 1] = lax.ppermute(parts[step], "fsdp", xor_pairs(members, 1))
        return [(me ^ step, parts[step]) for step in range(members)]

    def flat_pairs(target):
        pairs = []
        for i in range(members):
            for d in range(groups):
                role = (i % 2) ^ (d % 2)
                ti, td = target(i, d, role)
                pairs.append((i * groups + d, ti * groups + td))
        return pairs

    first_pairs = flat_pairs(lambda i, d, role: (i ^ (2 + 2 * role), d))
    relay_pairs = flat_pairs(lambda i, d, role: (i ^ (4 - 2 * role), d))
    partner_pairs = flat_pairs(lambda i, d, role: (i, d ^ 1))
    role = parity ^ (dp_index % 2)
    sibling = me ^ 1
    sibling_role = 1 - role
    sources = [me, me ^ (2 + 2 * role), me ^ 6, me ^ (4 - 2 * role)]
    sibling_sources = [sibling, sibling ^ (2 + 2 * sibling_role), sibling ^ 6,
                       sibling ^ (4 - 2 * sibling_role)]
    rows = shard.shape[0] // WEIGHT_CHUNKS
    result = []
    previous = None
    sibling_shard = lax.ppermute(shard, "fsdp", xor_pairs(members, 1))
    for k in range(WEIGHT_CHUNKS):
        piece = shard[k * rows:(k + 1) * rows]
        result.append((0.0, sources[0], k, piece))
        result.append((1.0, sibling_sources[0], k, sibling_shard[k * rows:(k + 1) * rows]))
        if previous is not None:
            piece, _ = lax.optimization_barrier((piece, previous))
        first = lax.ppermute(piece, ("fsdp", "dp"), first_pairs)
        previous = first
        result.append((2.0 + 2 * k, sources[1], k, first))
        if k + 1 == WEIGHT_CHUNKS:
            result.append((3.0 + 2 * k, sibling_sources[1], k,
                           lax.ppermute(first, "fsdp", xor_pairs(members, 1))))
        relayed = lax.ppermute(first, ("fsdp", "dp"), relay_pairs)
        partner = lax.ppermute(first, ("fsdp", "dp"), partner_pairs)
        result.append((4.5 + 2 * k, sources[2], k, relayed))
        result.append((4.5 + 2 * k, sources[3], k, partner))
        if k + 1 < WEIGHT_CHUNKS:
            late = lax.ppermute(jnp.stack([relayed, partner, first]), "fsdp", xor_pairs(members, 1))
            late_pieces = (late[0], late[1])
            result.append((5.5 + 2 * k, sibling_sources[1], k, late[2]))
        else:
            late_pieces = (lax.ppermute(relayed, "fsdp", xor_pairs(members, 1)),
                           lax.ppermute(partner, "fsdp", xor_pairs(members, 1)))
        result.append((5.5 + 2 * k, sibling_sources[2], k, late_pieces[0]))
        result.append((5.5 + 2 * k, sibling_sources[3], k, late_pieces[1]))
    result.sort(key=lambda item: item[0])
    return [item[1:] for item in result]


def on_device(
    tokens,
    output_gradient,
    frozen_value_weight,
    adapter_down_maps,
    adapter_up_maps,
    block_tenant_ids,
    block_live_rows,
    tenant_owner_slot,
):
    tok_rows, model_width = tokens.shape
    value_width = output_gradient.shape[1]
    blocks = block_tenant_ids.shape[0]
    block_length = tok_rows // blocks
    groups = lax.axis_size("dp")
    members = lax.axis_size("fsdp")
    shard_rows = frozen_value_weight.shape[0]
    me = lax.axis_index("fsdp")
    dp_index = lax.axis_index("dp")
    even_steps = list(range(2, members, 2))

    own_adapter = jnp.concatenate([adapter_down_maps[0], adapter_up_maps[0]], axis=1)
    by_step = {0: own_adapter}
    for step in even_steps:
        by_step[step] = lax.ppermute(own_adapter, "fsdp", xor_pairs(members, step))
    same_parity = jnp.stack([by_step[step] for step in range(0, members, 2)])
    other_parity = lax.ppermute(same_parity, "fsdp", xor_pairs(members, 1))
    for index, step in enumerate(range(0, members, 2)):
        by_step[step ^ 1] = other_parity[index]
    adapter_stack = jnp.stack([by_step[step] for step in range(members)])

    slot_ids = jnp.take(tenant_owner_slot, block_tenant_ids)
    member_ids = slot_ids // groups
    picked = jnp.stack([lax.dynamic_index_in_dim(adapter_stack, me ^ member_ids[b], 0, keepdims=False)
                        for b in range(blocks)])
    down_block = picked[:, :, :model_width]
    up_block = picked[:, :, model_width:]

    live_rows = (jnp.arange(block_length)[None, :] < block_live_rows[:, None]).astype(jnp.float32)
    live_column = live_rows[:, :, None]
    token_blocks = tokens.reshape(blocks, block_length, model_width)
    cot_blocks = output_gradient.reshape(blocks, block_length, value_width)

    low_rank_state = (
        jnp.einsum("cvj,coj->cvo", token_blocks, down_block, preferred_element_type=jnp.float32)
        * live_column
    ).astype(jnp.bfloat16)
    low_rank_gradient = (
        ADAPTER_SCALE
        * jnp.einsum("btv,bkv->btk", cot_blocks, up_block, preferred_element_type=jnp.float32)
        * live_column
    ).astype(jnp.bfloat16)

    partial_down = jnp.einsum(
        "vio,vih->voh", low_rank_gradient, token_blocks, preferred_element_type=jnp.float32
    )
    partial_up = ADAPTER_SCALE * jnp.einsum(
        "btk,btv->bkv", low_rank_state, cot_blocks, preferred_element_type=jnp.float32
    )
    partial = jnp.concatenate([partial_down, partial_up], axis=2)

    def table_row(member):
        row = jnp.zeros(partial.shape[1:], jnp.float32)
        for b in range(blocks):
            row = row + jnp.where(member_ids[b] == member, partial[b], 0.0)
        return row.astype(jnp.bfloat16)

    sibling = me ^ 1
    for_sibling = jnp.stack([table_row(sibling ^ step) for step in range(0, members, 2)])
    from_sibling = lax.ppermute(for_sibling, "fsdp", xor_pairs(members, 1))
    pair_sums = [
        table_row(me ^ step).astype(jnp.float32) + from_sibling[index].astype(jnp.float32)
        for index, step in enumerate(range(0, members, 2))
    ]
    weight_pieces = relay_gather(frozen_value_weight, members, groups, me, dp_index)
    if weight_pieces and len(weight_pieces[0]) == 2:
        weight_pieces = [(source, 0, value) for source, value in weight_pieces]
    last_pieces = (weight_pieces[-4][2],)
    grad_sum = pair_sums[0]
    for index, step in enumerate(even_steps):
        sent = pair_sums[index + 1].astype(jnp.bfloat16)
        sent, _ = lax.optimization_barrier((sent, last_pieces))
        grad_sum = grad_sum + lax.ppermute(sent, "fsdp", xor_pairs(members, step)).astype(jnp.float32)
    grad_sum = grad_sum.astype(jnp.bfloat16)
    grad_down = grad_sum[None, :, :model_width]
    grad_up = grad_sum[None, :, model_width:]

    adapter_output = jnp.einsum(
        "znr,zrm->znm", low_rank_state, up_block, preferred_element_type=jnp.float32
    ).reshape(tok_rows, value_width)
    live_flat = live_rows.reshape(tok_rows, 1)
    masked_cot = (output_gradient * live_flat).astype(jnp.bfloat16)

    output_total = ADAPTER_SCALE * adapter_output
    token_gradient = jnp.zeros((tok_rows, model_width), jnp.bfloat16)
    for source, chunk, weight_piece in weight_pieces:
        piece_rows = weight_piece.shape[0]
        column = source * shard_rows + chunk * piece_rows
        token_piece = lax.dynamic_slice_in_dim(tokens, column, piece_rows, axis=1)
        output_total = lax.optimization_barrier(output_total + jnp.dot(
            token_piece, weight_piece, preferred_element_type=jnp.float32
        ))
        down_piece = lax.dynamic_slice_in_dim(down_block, column, piece_rows, axis=2)
        backward_piece = lax.dot_general(
            masked_cot, weight_piece, (((1,), (1,)), ((), ())), preferred_element_type=jnp.float32
        ) + jnp.einsum(
            "uio,uof->uif", low_rank_gradient, down_piece, preferred_element_type=jnp.float32
        ).reshape(tok_rows, piece_rows)
        token_gradient = lax.dynamic_update_slice_in_dim(
            token_gradient, backward_piece.astype(jnp.bfloat16), column, axis=1
        )
    output = (live_flat * output_total).astype(jnp.bfloat16)
    return (output, token_gradient, grad_down, grad_up)


def solution(mesh):
    placed = (
        P(("fsdp", "dp"), None),
        P(("fsdp", "dp"), None),
        P("fsdp", None),
        P(("fsdp", "dp"), None, None),
        P(("fsdp", "dp"), None, None),
        P(("fsdp", "dp")),
        P(("fsdp", "dp")),
        P(),
    )
    return jax.shard_map(
        on_device,
        mesh=mesh,
        in_specs=placed,
        out_specs=(
            P(("fsdp", "dp"), None),
            P(("fsdp", "dp"), None),
            P(("fsdp", "dp"), None, None),
            P(("fsdp", "dp"), None, None),
        ),
        check_vma=False,
    )
```

```python
import jax
import jax.numpy as jnp
from jax import lax
from jax.sharding import PartitionSpec as P

ADAPTER_SCALE = 2.0
WEIGHT_CHUNKS = 2


def xor_pairs(count, step):
    return [(src, src ^ step) for src in range(count)]


def relay_gather(shard, members, groups, me, dp_index):
    flat = members * groups
    parity = me % 2
    if members != 8 or groups % 2 != 0:
        parts = {0: shard}
        for step in range(2, members, 2):
            parts[step] = lax.ppermute(shard, "fsdp", xor_pairs(members, step))
        for step in range(0, members, 2):
            parts[step + 1] = lax.ppermute(parts[step], "fsdp", xor_pairs(members, 1))
        return [(me ^ step, parts[step]) for step in range(members)]

    def flat_pairs(target):
        pairs = []
        for i in range(members):
            for d in range(groups):
                role = (i % 2) ^ (d % 2)
                ti, td = target(i, d, role)
                pairs.append((i * groups + d, ti * groups + td))
        return pairs

    first_pairs = flat_pairs(lambda i, d, role: (i ^ (2 + 2 * role), d))
    relay_pairs = flat_pairs(lambda i, d, role: (i ^ (4 - 2 * role), d))
    partner_pairs = flat_pairs(lambda i, d, role: (i, d ^ 1))
    role = parity ^ (dp_index % 2)
    sibling = me ^ 1
    sibling_role = 1 - role
    sources = [me, me ^ (2 + 2 * role), me ^ 6, me ^ (4 - 2 * role)]
    sibling_sources = [sibling, sibling ^ (2 + 2 * sibling_role), sibling ^ 6,
                       sibling ^ (4 - 2 * sibling_role)]
    rows = shard.shape[0] // WEIGHT_CHUNKS
    result = []
    previous = None
    for k in range(WEIGHT_CHUNKS):
        piece = shard[k * rows:(k + 1) * rows]
        result.append((0.0, sources[0], k, piece))
        if previous is not None:
            piece, _ = lax.optimization_barrier((piece, previous))
        first = lax.ppermute(piece, ("fsdp", "dp"), first_pairs)
        if previous is None:
            held, _ = lax.optimization_barrier((shard, first))
            sibling_shard = lax.ppermute(held, "fsdp", xor_pairs(members, 1))
            for j in range(WEIGHT_CHUNKS):
                result.append((2.5, sibling_sources[0], j, sibling_shard[j * rows:(j + 1) * rows]))
        previous = first
        result.append((2.0 + 2 * k, sources[1], k, first))
        result.append((3.0 + 2 * k, sibling_sources[1], k, lax.ppermute(first, "fsdp", xor_pairs(members, 1))))
        relayed = lax.ppermute(first, ("fsdp", "dp"), relay_pairs)
        partner = lax.ppermute(first, ("fsdp", "dp"), partner_pairs)
        result.append((4.5 + 2 * k, sources[2], k, relayed))
        result.append((4.5 + 2 * k, sources[3], k, partner))
        if k + 1 < WEIGHT_CHUNKS:
            late = lax.ppermute(jnp.stack([relayed, partner]), "fsdp", xor_pairs(members, 1))
            late_pieces = (late[0], late[1])
        else:
            late_pieces = (lax.ppermute(relayed, "fsdp", xor_pairs(members, 1)),
                           lax.ppermute(partner, "fsdp", xor_pairs(members, 1)))
        result.append((5.5 + 2 * k, sibling_sources[2], k, late_pieces[0]))
        result.append((5.5 + 2 * k, sibling_sources[3], k, late_pieces[1]))
    result.sort(key=lambda item: item[0])
    return [item[1:] for item in result]


def on_device(
    tokens,
    output_gradient,
    frozen_value_weight,
    adapter_down_maps,
    adapter_up_maps,
    block_tenant_ids,
    block_live_rows,
    tenant_owner_slot,
):
    tok_rows, model_width = tokens.shape
    value_width = output_gradient.shape[1]
    blocks = block_tenant_ids.shape[0]
    block_length = tok_rows // blocks
    groups = lax.axis_size("dp")
    members = lax.axis_size("fsdp")
    shard_rows = frozen_value_weight.shape[0]
    me = lax.axis_index("fsdp")
    dp_index = lax.axis_index("dp")
    even_steps = list(range(2, members, 2))

    own_adapter = jnp.concatenate([adapter_down_maps[0], adapter_up_maps[0]], axis=1)
    by_step = {0: own_adapter}
    for step in even_steps:
        by_step[step] = lax.ppermute(own_adapter, "fsdp", xor_pairs(members, step))
    same_parity = jnp.stack([by_step[step] for step in range(0, members, 2)])
    other_parity = lax.ppermute(same_parity, "fsdp", xor_pairs(members, 1))
    for index, step in enumerate(range(0, members, 2)):
        by_step[step ^ 1] = other_parity[index]
    adapter_stack = jnp.stack([by_step[step] for step in range(members)])

    slot_ids = jnp.take(tenant_owner_slot, block_tenant_ids)
    member_ids = slot_ids // groups
    picked = jnp.stack([lax.dynamic_index_in_dim(adapter_stack, me ^ member_ids[b], 0, keepdims=False)
                        for b in range(blocks)])
    down_block = picked[:, :, :model_width]
    up_block = picked[:, :, model_width:]

    live_rows = (jnp.arange(block_length)[None, :] < block_live_rows[:, None]).astype(jnp.float32)
    live_column = live_rows[:, :, None]
    token_blocks = tokens.reshape(blocks, block_length, model_width)
    cot_blocks = output_gradient.reshape(blocks, block_length, value_width)

    low_rank_state = (
        jnp.einsum("cvj,coj->cvo", token_blocks, down_block, preferred_element_type=jnp.float32)
        * live_column
    ).astype(jnp.bfloat16)
    low_rank_gradient = (
        ADAPTER_SCALE
        * jnp.einsum("btv,bkv->btk", cot_blocks, up_block, preferred_element_type=jnp.float32)
        * live_column
    ).astype(jnp.bfloat16)

    partial_down = jnp.einsum(
        "vio,vih->voh", low_rank_gradient, token_blocks, preferred_element_type=jnp.float32
    )
    partial_up = ADAPTER_SCALE * jnp.einsum(
        "btk,btv->bkv", low_rank_state, cot_blocks, preferred_element_type=jnp.float32
    )
    partial = jnp.concatenate([partial_down, partial_up], axis=2)

    def table_row(member):
        row = jnp.zeros(partial.shape[1:], jnp.float32)
        for b in range(blocks):
            row = row + jnp.where(member_ids[b] == member, partial[b], 0.0)
        return row.astype(jnp.bfloat16)

    sibling = me ^ 1
    for_sibling = jnp.stack([table_row(sibling ^ step) for step in range(0, members, 2)])
    from_sibling = lax.ppermute(for_sibling, "fsdp", xor_pairs(members, 1))
    pair_sums = [
        table_row(me ^ step).astype(jnp.float32) + from_sibling[index].astype(jnp.float32)
        for index, step in enumerate(range(0, members, 2))
    ]
    weight_pieces = relay_gather(frozen_value_weight, members, groups, me, dp_index)
    if weight_pieces and len(weight_pieces[0]) == 2:
        weight_pieces = [(source, 0, value) for source, value in weight_pieces]
    last_pieces = (weight_pieces[-4][2],)
    grad_sum = pair_sums[0]
    for index, step in enumerate(even_steps):
        sent = pair_sums[index + 1].astype(jnp.bfloat16)
        sent, _ = lax.optimization_barrier((sent, last_pieces))
        grad_sum = grad_sum + lax.ppermute(sent, "fsdp", xor_pairs(members, step)).astype(jnp.float32)
    grad_sum = grad_sum.astype(jnp.bfloat16)
    grad_down = grad_sum[None, :, :model_width]
    grad_up = grad_sum[None, :, model_width:]

    adapter_output = jnp.einsum(
        "znr,zrm->znm", low_rank_state, up_block, preferred_element_type=jnp.float32
    ).reshape(tok_rows, value_width)
    live_flat = live_rows.reshape(tok_rows, 1)
    masked_cot = (output_gradient * live_flat).astype(jnp.bfloat16)

    output_total = ADAPTER_SCALE * adapter_output
    token_gradient = jnp.zeros((tok_rows, model_width), jnp.bfloat16)
    for source, chunk, weight_piece in weight_pieces:
        piece_rows = weight_piece.shape[0]
        column = source * shard_rows + chunk * piece_rows
        token_piece = lax.dynamic_slice_in_dim(tokens, column, piece_rows, axis=1)
        output_total = lax.optimization_barrier(output_total + jnp.dot(
            token_piece, weight_piece, preferred_element_type=jnp.float32
        ))
        down_piece = lax.dynamic_slice_in_dim(down_block, column, piece_rows, axis=2)
        backward_piece = lax.dot_general(
            masked_cot, weight_piece, (((1,), (1,)), ((), ())), preferred_element_type=jnp.float32
        ) + jnp.einsum(
            "uio,uof->uif", low_rank_gradient, down_piece, preferred_element_type=jnp.float32
        ).reshape(tok_rows, piece_rows)
        token_gradient = lax.dynamic_update_slice_in_dim(
            token_gradient, backward_piece.astype(jnp.bfloat16), column, axis=1
        )
    output = (live_flat * output_total).astype(jnp.bfloat16)
    return (output, token_gradient, grad_down, grad_up)


def solution(mesh):
    placed = (
        P(("fsdp", "dp"), None),
        P(("fsdp", "dp"), None),
        P("fsdp", None),
        P(("fsdp", "dp"), None, None),
        P(("fsdp", "dp"), None, None),
        P(("fsdp", "dp")),
        P(("fsdp", "dp")),
        P(),
    )
    return jax.shard_map(
        on_device,
        mesh=mesh,
        in_specs=placed,
        out_specs=(
            P(("fsdp", "dp"), None),
            P(("fsdp", "dp"), None),
            P(("fsdp", "dp"), None, None),
            P(("fsdp", "dp"), None, None),
        ),
        check_vma=False,
    )
```
